512 devices in a mesh: gx: 16 (over y_hi, x, core), gy: 32 (over z, y_lo).
Axes of the slice: x: 4, y: 4 (y_hi: 2, y_lo: 2; y = y_hi * 2 + y_lo), z: 16, core: 2. Of those that a mesh axis runs over, the one named last changes fastest.
Arguments:
- e_field: float32 [3, 64, 128, 2048], P(None, 'gx', 'gy'), may hold values from -6 to 6
- h_field: float32 [3, 64, 128, 2048], P(None, 'gx', 'gy'), may hold values from -6 to 6
- polarization: float32 [4, 3, 64, 128, 2048], P(None, None, 'gx', 'gy'), may hold values from -3 to 3
- material: int32 [64, 128, 2048], P('gx', 'gy'), may hold values from 0 to 7
- eps_inf: float32 [8], replicated, may hold values from 3 to 12
- conductivity: float32 [8], replicated, may hold values from 0.05 to 1
- pole_strength: float32 [4, 8], replicated, may hold values from 0.1 to 1
- pole_decay: float32 [4, 8], replicated, may hold values from 0.2 to 0.95
- seg_owner: int32 [16, 16384, 1], P('gx', 'gy'), may hold values from 0 to 31; in each aligned block of 512 rows (0 to 511, 512 to 1023, ..., all dimensions but the last counted through in order) at most 32 rows name the same one
- seg_cell: int32 [16, 16384], P('gx', 'gy'), may hold values from 0 to 32767
- current: float32 [16, 16384], P('gx', 'gy'), may hold values from -6 to 6
- voltage: float32 [16, 16384], P('gx', 'gy'), may hold values from -6 to 6
- wire_gain: float32 [16, 16384], P('gx', 'gy'), may hold values from 0.05 to 0.5
- wire_cap: float32 [16, 16384], P('gx', 'gy'), may hold values from 0.05 to 0.5
Outputs:
- e_field_out: float32 [3, 64, 128, 2048], P(None, 'gx', 'gy')
- h_field_out: float32 [3, 64, 128, 2048], P(None, 'gx', 'gy')
- polarization_out: float32 [4, 3, 64, 128, 2048], P(None, None, 'gx', 'gy')
- current_out: float32 [16, 16384], P('gx', 'gy')
- voltage_out: float32 [16, 16384], P('gx', 'gy')
The draws below stay inside these ranges and needn't reach their ends.
Inputs may be any that keep to these rules, and one draw needn't show every extreme that they name: `seg_owner`: in each aligned block of 512 rows (the segments of one device), no column is named by more than 32 rows, a bound that some block reaches.
All inputs are finite; a program needn't handle non-finite values.
Results may differ from the reference program's by a relative error of at most 0.0001.
Values sent between devices are 32-bit elements; how exact they have to be, the bound alone decides.
No kernel may reach another device: no remote copies, remote signals or barrier semaphores. Data moves between devices by JAX's collectives and lax.ppermute only.
A program may use at most 64 MiB of HBM per device.

```python
import math
import jax
import jax.numpy as jnp
import numpy as np
from jax import lax

CX = 4
CY = 4
CZ = 2048
SEG = 512
STEPS = 2
POLES = 4
MATS = 8
CAP = 32
CELLS = 32768
NX = 64
NY = 128
N_GX = 16
N_GY = 32


def set_ends(result, stream_key, smallest, largest):
    longest = result.shape.index(max(result.shape))
    spots = []
    for shift in (0, 1):
        where = [jax.random.randint(jax.random.fold_in(stream_key, axis), (), 0, length) for axis, length in enumerate(result.shape)]
        where[longest] = (where[longest] + shift) % result.shape[longest]
        spots.append(tuple(where))
    return result.at[spots[0]].set(smallest).at[spots[1]].set(largest)


def block_scale(stream_key, shape, cuts, smallest, top_value):
    level, own = 1.0, jax.random.fold_in(stream_key, 6)
    for dim, shards_of in cuts:
        draws = jnp.exp(jax.random.uniform(jax.random.fold_in(own, dim), (shards_of,), jnp.float32, smallest / len(cuts), top_value / len(cuts)))
        level = level * jnp.repeat(draws, shape[dim] // shards_of).reshape([-1 if axis == dim else 1 for axis in range(len(shape))])
    return level


def assign_block(stream_key, own, number, rows, amount, top, bound, skew):
    ranking = jax.random.permutation(stream_key, amount)
    heavy_load, common = portions_of(amount, rows * top, bound, skew, True), portions_of(amount, rows * top, bound, skew, False)
    places = jnp.arange(amount)

    def named(tallies, offset_by):
        used = int((tallies > 0).sum())
        fixed = max(1, used // 4)
        shifted = fixed + (places - fixed + offset_by * (used - fixed)) % max(1, amount - fixed)
        return jnp.zeros((amount,), jnp.int32).at[ranking[jnp.where(places < fixed, places, shifted)]].set(jnp.asarray(tallies, jnp.int32))

    tallies = jnp.where(number % 4 == 0, named(heavy_load, number // 4), named(common, number - number // 4 - 1))
    mixed = jax.random.permutation(jax.random.fold_in(own, 3), amount)
    giver, receiver = mixed[0:amount // 2 * 2:2], mixed[1:amount // 2 * 2:2]
    slack = jnp.minimum(tallies[giver] - 1, bound - tallies[receiver]) // 2
    slack = jnp.where((giver == ranking[0]) | (receiver == ranking[0]) | (tallies[receiver] == 0), 0, jnp.maximum(slack, 0))
    shifted = jax.random.randint(jax.random.fold_in(own, 4), (amount // 2,), 0, 1 << 20) % (slack + 1)
    tallies = tallies.at[giver].add(-shifted).at[receiver].add(shifted)
    members = jnp.searchsorted(jnp.cumsum(tallies), jnp.arange(rows * top), side="right").astype(jnp.int32)
    table = members.reshape(top, rows).T
    table = table[jax.random.permutation(jax.random.fold_in(own, 1), rows)]
    offset_by = jax.random.randint(jax.random.fold_in(own, 2), (rows, 1), 0, top)
    return jnp.take_along_axis(table, (jnp.arange(top)[None, :] + offset_by) % top, axis=1)


def portions_of(amount, total, reach, slope, full):
    portions = [(1 << 20) // math.isqrt(grade ** slope) + 1 for grade in range(1, amount + 1)]
    largest = reach if full else min(reach, max(-(-total // amount), total * portions[0] // sum(portions)))
    least = 1 if total - largest >= amount - 1 else 0
    counts, spare = [largest] + [least] * (amount - 1), total - largest - least * (amount - 1)
    while spare > 0:
        movable = [i for i in range(1, amount) if counts[i] < largest] or [i for i in range(1, amount) if counts[i] < reach]
        pool, remaining = sum([portions[i] for i in movable]), spare
        for i in movable:
            addition = min(reach - counts[i], max(1, remaining * portions[i] // pool), spare)
            counts[i] = counts[i] + addition
            spare = spare - addition
    return np.array(counts)


def noise(own_key, dims, width, reach, split=(), held_as=jnp.bfloat16):
    level = block_scale(own_key, dims, split, -0.22, 0.18) if split else 1.0
    entries = jax.random.normal(own_key, dims, jnp.float32) * width * level
    return jnp.minimum(jnp.maximum(entries, -reach), reach).astype(held_as)


def setup_inputs(seed: int = 0) -> dict:
    splits = jax.random.split(jax.random.key(seed), 15)
    e_field = noise(splits[0], (3, NX, NY, CZ), 1.0, 6.0, ((1, 16), (2, 32)), jnp.float32)
    h_field = noise(splits[1], (3, NX, NY, CZ), 1.0, 6.0, ((1, 16), (2, 32)), jnp.float32)
    polarization = noise(splits[2], (POLES, 3, NX, NY, CZ), 0.5, 3.0, ((2, 16), (3, 32)), jnp.float32)
    material = set_ends(jax.random.randint(splits[3], (NX, NY, CZ), 0, MATS), jax.random.fold_in(splits[3], 1), 0, MATS - 1).astype(jnp.int32)
    eps_inf = jnp.clip(jax.random.uniform(splits[4], (MATS,), jnp.float32, 3.0, 12.0), 3.0, 12.0)
    conductivity = jnp.clip(jax.random.uniform(splits[5], (MATS,), jnp.float32, 0.05, 1.0), 0.05, 1.0)
    pole_strength = jnp.clip(jax.random.uniform(splits[6], (POLES, MATS), jnp.float32, 0.1, 1.0), 0.1, 1.0)
    pole_decay = jnp.clip(jax.random.uniform(splits[7], (POLES, MATS), jnp.float32, 0.2, 0.95), 0.2, 0.95)
    seg_owner_keys = jax.random.split(jax.random.fold_in(splits[8], 1), N_GX * (N_GY * SEG) // SEG)
    seg_owner_turns = jax.random.permutation(jax.random.fold_in(splits[8], 3), N_GX * (N_GY * SEG) // SEG)
    seg_owner = jax.vmap(lambda own, number: assign_block(jax.random.fold_in(splits[8], 2), own, number, SEG, N_GY, 1, CAP, 2))(seg_owner_keys, seg_owner_turns).reshape((N_GX, N_GY * SEG, 1))
    seg_cell = set_ends(jax.random.randint(splits[9], (N_GX, N_GY * SEG), 0, CELLS), jax.random.fold_in(splits[9], 1), 0, CELLS - 1).astype(jnp.int32)
    current = noise(splits[10], (N_GX, N_GY * SEG), 1.0, 6.0, ((0, 16), (1, 32)), jnp.float32)
    voltage = noise(splits[11], (N_GX, N_GY * SEG), 1.0, 6.0, ((0, 16), (1, 32)), jnp.float32)
    wire_gain = jnp.clip(jnp.exp(math.log(0.5) - 2.3025851 * jax.random.uniform(splits[12], (N_GX, N_GY * SEG), jnp.float32) ** block_scale(splits[12], (N_GX, N_GY * SEG), ((0, 16), (1, 32)), -0.2, 0.2)), 0.05, 0.5)
    wire_cap = jnp.clip(jnp.exp(math.log(0.5) - 2.3025851 * jax.random.uniform(splits[13], (N_GX, N_GY * SEG), jnp.float32) ** block_scale(splits[13], (N_GX, N_GY * SEG), ((0, 16), (1, 32)), -0.2, 0.2)), 0.05, 0.5)
    return dict(e_field=e_field, h_field=h_field, polarization=polarization, material=material, eps_inf=eps_inf, conductivity=conductivity, pole_strength=pole_strength, pole_decay=pole_decay, seg_owner=seg_owner, seg_cell=seg_cell, current=current, voltage=voltage, wire_gain=wire_gain, wire_cap=wire_cap)


TIME_STEP = 0.5


def step_up(field, dim_index):
    extent = field.shape[dim_index]
    kept_part = lax.slice_in_dim(field, 1, extent, axis=dim_index)
    zero_part = jnp.zeros_like(lax.slice_in_dim(field, 0, 1, axis=dim_index))
    return jnp.concatenate([kept_part, zero_part], axis=dim_index)


def step_down(field, dim_index):
    extent = field.shape[dim_index]
    kept_part = lax.slice_in_dim(field, 0, extent - 1, axis=dim_index)
    zero_part = jnp.zeros_like(lax.slice_in_dim(field, 0, 1, axis=dim_index))
    return jnp.concatenate([zero_part, kept_part], axis=dim_index)


def reference(e_field, h_field, polarization, material, eps_inf, conductivity, pole_strength, pole_decay, seg_owner, seg_cell, current, voltage, wire_gain, wire_cap):
    eps_cell = eps_inf[material]
    sigma_cell = conductivity[material]
    strength_cell = pole_strength[:, material]
    decay_cell = pole_decay[:, material]
    owner_col = seg_owner[:, :, 0]
    row_index = jnp.arange(N_GX, dtype=jnp.int32)[:, None]
    x_index = row_index * CX + seg_cell // (CY * CZ)
    y_index = owner_col * CY + (seg_cell // CZ) % CY
    z_index = seg_cell % CZ
    wire_gain3 = wire_gain.reshape(N_GX, N_GY, SEG)
    wire_cap3 = wire_cap.reshape(N_GX, N_GY, SEG)
    for step_index in range(STEPS):
        elec_x, elec_y, elec_z = e_field[0], e_field[1], e_field[2]
        magn_x = h_field[0] - TIME_STEP * ((step_up(elec_z, 1) - elec_z) - (step_up(elec_y, 2) - elec_y))
        magn_y = h_field[1] - TIME_STEP * ((step_up(elec_x, 2) - elec_x) - (step_up(elec_z, 0) - elec_z))
        magn_z = h_field[2] - TIME_STEP * ((step_up(elec_y, 0) - elec_y) - (step_up(elec_x, 1) - elec_x))
        h_field = jnp.stack([magn_x, magn_y, magn_z])
        seg_sample = elec_z[x_index, y_index, z_index].reshape(N_GX, N_GY, SEG)
        volt_now = voltage.reshape(N_GX, N_GY, SEG)
        curr_now = current.reshape(N_GX, N_GY, SEG)
        volt_next = step_up(volt_now, 2)
        curr_now = curr_now + wire_gain3 * (seg_sample - (volt_next - volt_now))
        curr_prev = step_down(curr_now, 2)
        volt_now = volt_now - wire_cap3 * (curr_now - curr_prev)
        current = curr_now.reshape(N_GX, N_GY * SEG)
        voltage = volt_now.reshape(N_GX, N_GY * SEG)
        wire_term = jnp.zeros((NX, NY, CZ), jnp.float32).at[x_index, y_index, z_index].add(current)
        curl_x = (magn_z - step_down(magn_z, 1)) - (magn_y - step_down(magn_y, 2))
        curl_y = (magn_x - step_down(magn_x, 2)) - (magn_z - step_down(magn_z, 0))
        curl_z = (magn_y - step_down(magn_y, 0)) - (magn_x - step_down(magn_x, 1))
        curl_all = jnp.stack([curl_x, curl_y, curl_z])
        polar_new = decay_cell[:, None] * polarization + (1.0 - decay_cell[:, None]) * strength_cell[:, None] * e_field[None]
        change = jnp.sum(polar_new - polarization, axis=0)
        drive = TIME_STEP * curl_all - TIME_STEP * sigma_cell[None] * e_field - change
        drive = drive.at[2].add(-TIME_STEP * wire_term)
        e_field = e_field + drive / eps_cell[None]
        polarization = polar_new
    return e_field, h_field, polarization, current, voltage
```

```python
import jax
import jax.numpy as jnp
from jax import lax
from jax.sharding import PartitionSpec as P

STEPS = 2


TIME_STEP = 0.5


def passed_along(value, axis, steps):
    count = lax.axis_size(axis)
    first, last = (max(0, -steps), min(count, count - steps))
    return lax.ppermute(value, axis, [(source, source + steps) for source in range(first, last)])


def next_vertical(field):
    return jnp.concatenate([field[..., 1:], jnp.zeros_like(field[..., :1])], axis=-1)


def prev_vertical(field):
    return jnp.concatenate([jnp.zeros_like(field[..., :1]), field[..., :-1]], axis=-1)


def electric_rims(e_field):
    face_x = passed_along(e_field[1:3, :1], "gx", -1)
    plus_x = jnp.concatenate([e_field[1:3, 1:], face_x], axis=1)
    face_y = passed_along(e_field[0::2, :, :1], "gy", -1)
    plus_y = jnp.concatenate([e_field[0::2, :, 1:], face_y], axis=2)
    return (plus_x, plus_y)


def magnetic_rims(h_field):
    face_x = passed_along(h_field[1:3, -1:], "gx", 1)
    minus_x = jnp.concatenate([face_x, h_field[1:3, :-1]], axis=1)
    face_y = passed_along(h_field[0::2, :, -1:], "gy", 1)
    minus_y = jnp.concatenate([face_y, h_field[0::2, :, :-1]], axis=2)
    return (minus_x, minus_y)


def magnetic_update(e_field, h_field):
    plus_x, plus_y = electric_rims(e_field)
    elec_x, elec_y, elec_z = (e_field[0], e_field[1], e_field[2])
    magn_x = h_field[0] - TIME_STEP * (plus_y[1] - elec_z - (next_vertical(elec_y) - elec_y))
    magn_y = h_field[1] - TIME_STEP * (next_vertical(elec_x) - elec_x - (plus_x[1] - elec_z))
    magn_z = h_field[2] - TIME_STEP * (plus_x[0] - elec_y - (plus_y[0] - elec_x))
    return jnp.stack([magn_x, magn_y, magn_z])


def electric_update(e_field, h_field, polarization, wire_term, cells):
    eps_cell, sigma_cell, strength_cell, decay_cell = cells
    magn_x, magn_y, magn_z = (h_field[0], h_field[1], h_field[2])
    minus_x, minus_y = magnetic_rims(h_field)
    curl_x = magn_z - minus_y[1] - (magn_y - prev_vertical(magn_y))
    curl_y = magn_x - prev_vertical(magn_x) - (magn_z - minus_x[1])
    curl_z = magn_y - minus_x[0] - (magn_x - minus_y[0])
    curl_all = jnp.stack([curl_x, curl_y, curl_z])
    polar_new = (
        decay_cell[:, None] * polarization
        + (1.0 - decay_cell[:, None]) * strength_cell[:, None] * e_field[None]
    )
    change = jnp.sum(polar_new - polarization, axis=0)
    drive = TIME_STEP * curl_all - TIME_STEP * sigma_cell[None] * e_field - change
    drive = drive.at[2].add(-TIME_STEP * wire_term)
    return (e_field + drive / eps_cell[None], polar_new)


def on_device(
    e_field,
    h_field,
    polarization,
    material,
    eps_inf,
    conductivity,
    pole_strength,
    pole_decay,
    seg_owner,
    seg_cell,
    current,
    voltage,
    wire_gain,
    wire_cap,
):
    n_gy = lax.axis_size("gy")
    seg_count = seg_owner.shape[1]
    capacity = max(2 * seg_count // n_gy, 16)
    owner_col = seg_owner[0, :, 0]
    cell_ids = seg_cell[0]
    owner_hot = (owner_col[:, None] == jnp.arange(n_gy, dtype=jnp.int32)[None, :]).astype(jnp.int32)
    rank_in = jnp.sum((jnp.cumsum(owner_hot, axis=0) - 1) * owner_hot, axis=1)
    slot_at = owner_col * capacity + rank_in
    grid_shape = material.shape
    cell_total = grid_shape[0] * grid_shape[1] * grid_shape[2]
    single_zero = jnp.zeros((1,), jnp.float32)

    def to_slots(rows, fill):
        empty = jnp.broadcast_to(jnp.asarray(fill, jnp.float32)[:, None], (rows.shape[0], n_gy * capacity))
        buffer = empty.at[:, slot_at].set(rows)
        return buffer.reshape(rows.shape[0], n_gy, capacity).transpose(1, 0, 2)

    def exchange(blocks):
        return lax.all_to_all(blocks, "gy", split_axis=0, concat_axis=0, tiled=True)

    def from_slots(blocks):
        flat = blocks.transpose(1, 0, 2).reshape(blocks.shape[1], n_gy * capacity)
        return flat[:, slot_at]

    gain_row = wire_gain[0]
    cap_row = wire_cap[0]
    volt_0 = voltage[0]
    curr_0 = current[0]
    drop_0 = jnp.concatenate([volt_0[1:], single_zero]) - volt_0
    outgoing = to_slots(jnp.stack([cell_ids.astype(jnp.float32), curr_0, gain_row, drop_0]), [-1.0, 0.0, 0.0, 0.0])
    incoming = exchange(outgoing)
    recv_cells = incoming[:, 0, :].astype(jnp.int32)
    is_valid = recv_cells >= 0
    safe_cells = jnp.where(is_valid, recv_cells, 0).reshape(-1)
    recv_curr = incoming[:, 1, :].reshape(-1)
    recv_gain = incoming[:, 2, :].reshape(-1)
    recv_drop = incoming[:, 3, :].reshape(-1)
    valid_flat = is_valid.reshape(-1)

    material_hot = (
        material[None] == jnp.arange(eps_inf.shape[0], dtype=jnp.int32)[:, None, None, None]
    ).astype(jnp.float32)
    highest = lax.Precision.HIGHEST
    eps_cell = jnp.einsum("m,mxyz->xyz", eps_inf, material_hot, precision=highest)
    sigma_cell = jnp.einsum("m,mxyz->xyz", conductivity, material_hot, precision=highest)
    strength_cell = jnp.einsum("pm,mxyz->pxyz", pole_strength, material_hot, precision=highest)
    decay_cell = jnp.einsum("pm,mxyz->pxyz", pole_decay, material_hot, precision=highest)
    cells = (eps_cell, sigma_cell, strength_cell, decay_cell)

    def sample(e_now):
        return jnp.where(valid_flat, e_now[2].reshape(-1)[safe_cells], 0.0)

    def wire_of(values):
        return jnp.zeros((cell_total,), jnp.float32).at[safe_cells].add(values).reshape(grid_shape)

    sample_0 = sample(e_field)
    h_field = magnetic_update(e_field, h_field)
    curr_cell_1 = recv_curr + recv_gain * (sample_0 - recv_drop)
    e_field, polarization = electric_update(e_field, h_field, polarization, wire_of(curr_cell_1), cells)
    sample_1 = sample(e_field)

    returned = from_slots(exchange(jnp.stack([sample_0, sample_1]).reshape(2, n_gy, capacity).transpose(1, 0, 2)))
    seg_sample_0, seg_sample_1 = returned[0], returned[1]
    curr_1 = curr_0 + gain_row * (seg_sample_0 - drop_0)
    curr_prev = jnp.concatenate([single_zero, curr_1[:-1]])
    volt_1 = volt_0 - cap_row * (curr_1 - curr_prev)
    drop_1 = jnp.concatenate([volt_1[1:], single_zero]) - volt_1
    curr_2 = curr_1 + gain_row * (seg_sample_1 - drop_1)
    curr_prev = jnp.concatenate([single_zero, curr_2[:-1]])
    volt_2 = volt_1 - cap_row * (curr_2 - curr_prev)

    h_field = magnetic_update(e_field, h_field)
    recv_curr_2 = exchange(to_slots(curr_2[None], [0.0])).transpose(1, 0, 2).reshape(-1)
    e_field, polarization = electric_update(e_field, h_field, polarization, wire_of(recv_curr_2), cells)
    return (e_field, h_field, polarization, curr_2[None], volt_2[None])


def solution(mesh):
    return jax.shard_map(
        on_device,
        mesh=mesh,
        in_specs=(
            P(None, "gx", "gy", None),
            P(None, "gx", "gy", None),
            P(None, None, "gx", "gy", None),
            P("gx", "gy", None),
            P(),
            P(),
            P(),
            P(),
            P("gx", "gy", None),
            P("gx", "gy"),
            P("gx", "gy"),
            P("gx", "gy"),
            P("gx", "gy"),
            P("gx", "gy"),
        ),
        out_specs=(
            P(None, "gx", "gy", None),
            P(None, "gx", "gy", None),
            P(None, None, "gx", "gy", None),
            P("gx", "gy"),
            P("gx", "gy"),
        ),
        check_vma=False,
    )
```

```python
import jax
import jax.numpy as jnp
from jax import lax
from jax.sharding import PartitionSpec as P

STEPS = 2


TIME_STEP = 0.5


def passed_along(value, axis, steps):
    count = lax.axis_size(axis)
    first, last = (max(0, -steps), min(count, count - steps))
    return lax.ppermute(value, axis, [(source, source + steps) for source in range(first, last)])


def next_vertical(field):
    return jnp.concatenate([field[..., 1:], jnp.zeros_like(field[..., :1])], axis=-1)


def prev_vertical(field):
    return jnp.concatenate([jnp.zeros_like(field[..., :1]), field[..., :-1]], axis=-1)


def electric_rims(e_field):
    face_x = passed_along(e_field[1:3, :1], "gx", -1)
    plus_x = jnp.concatenate([e_field[1:3, 1:], face_x], axis=1)
    face_y = passed_along(e_field[0::2, :, :1], "gy", -1)
    plus_y = jnp.concatenate([e_field[0::2, :, 1:], face_y], axis=2)
    return (plus_x, plus_y)


def magnetic_rims(h_field):
    face_x = passed_along(h_field[1:3, -1:], "gx", 1)
    minus_x = jnp.concatenate([face_x, h_field[1:3, :-1]], axis=1)
    face_y = passed_along(h_field[0::2, :, -1:], "gy", 1)
    minus_y = jnp.concatenate([face_y, h_field[0::2, :, :-1]], axis=2)
    return (minus_x, minus_y)


def magnetic_update(e_field, h_field):
    plus_x, plus_y = electric_rims(e_field)
    elec_x, elec_y, elec_z = (e_field[0], e_field[1], e_field[2])
    magn_x = h_field[0] - TIME_STEP * (plus_y[1] - elec_z - (next_vertical(elec_y) - elec_y))
    magn_y = h_field[1] - TIME_STEP * (next_vertical(elec_x) - elec_x - (plus_x[1] - elec_z))
    magn_z = h_field[2] - TIME_STEP * (plus_x[0] - elec_y - (plus_y[0] - elec_x))
    return jnp.stack([magn_x, magn_y, magn_z])


def electric_update(e_field, h_field, polarization, wire_term, cells):
    eps_cell, sigma_cell, strength_cell, decay_cell = cells
    magn_x, magn_y, magn_z = (h_field[0], h_field[1], h_field[2])
    minus_x, minus_y = magnetic_rims(h_field)
    curl_x = magn_z - minus_y[1] - (magn_y - prev_vertical(magn_y))
    curl_y = magn_x - prev_vertical(magn_x) - (magn_z - minus_x[1])
    curl_z = magn_y - minus_x[0] - (magn_x - minus_y[0])
    curl_all = jnp.stack([curl_x, curl_y, curl_z])
    polar_new = (
        decay_cell[:, None] * polarization
        + (1.0 - decay_cell[:, None]) * strength_cell[:, None] * e_field[None]
    )
    change = jnp.sum(polar_new - polarization, axis=0)
    drive = TIME_STEP * curl_all - TIME_STEP * sigma_cell[None] * e_field - change
    drive = drive.at[2].add(-TIME_STEP * wire_term)
    return (e_field + drive / eps_cell[None], polar_new)


def on_device(
    e_field,
    h_field,
    polarization,
    material,
    eps_inf,
    conductivity,
    pole_strength,
    pole_decay,
    seg_owner,
    seg_cell,
    current,
    voltage,
    wire_gain,
    wire_cap,
):
    n_gy = lax.axis_size("gy")
    seg_count = seg_owner.shape[1]
    capacity = max(2 * seg_count // n_gy, 16)
    owner_col = seg_owner[0, :, 0]
    cell_ids = seg_cell[0]
    owner_hot = (owner_col[:, None] == jnp.arange(n_gy, dtype=jnp.int32)[None, :]).astype(jnp.int32)
    rank_in = jnp.sum((jnp.cumsum(owner_hot, axis=0) - 1) * owner_hot, axis=1)
    slot_at = owner_col * capacity + rank_in
    grid_shape = material.shape
    cell_total = grid_shape[0] * grid_shape[1] * grid_shape[2]
    single_zero = jnp.zeros((1,), jnp.float32)

    slot_total = n_gy * capacity
    highest = lax.Precision.HIGHEST
    slot_hot = (jnp.arange(slot_total, dtype=jnp.int32)[:, None] == slot_at[None, :]).astype(jnp.float32)
    slot_used = jnp.sum(slot_hot, axis=1)

    def to_slots(rows, fill):
        placed = jnp.einsum("fs,ts->ft", rows, slot_hot, precision=highest)
        buffer = placed + jnp.asarray(fill, jnp.float32)[:, None] * (1.0 - slot_used)[None, :]
        return buffer.reshape(rows.shape[0], n_gy, capacity).transpose(1, 0, 2)

    def exchange(blocks):
        return lax.all_to_all(blocks, "gy", split_axis=0, concat_axis=0, tiled=True)

    def from_slots(blocks):
        flat = blocks.transpose(1, 0, 2).reshape(blocks.shape[1], slot_total)
        return jnp.einsum("ft,ts->fs", flat, slot_hot, precision=highest)

    gain_row = wire_gain[0]
    cap_row = wire_cap[0]
    volt_0 = voltage[0]
    curr_0 = current[0]
    drop_0 = jnp.concatenate([volt_0[1:], single_zero]) - volt_0
    outgoing = to_slots(jnp.stack([cell_ids.astype(jnp.float32), curr_0, gain_row, drop_0]), [-1.0, 0.0, 0.0, 0.0])
    incoming = exchange(outgoing)
    recv_cells = incoming[:, 0, :].astype(jnp.int32)
    is_valid = recv_cells >= 0
    safe_cells = jnp.where(is_valid, recv_cells, 0).reshape(-1)
    recv_curr = incoming[:, 1, :].reshape(-1)
    recv_gain = incoming[:, 2, :].reshape(-1)
    recv_drop = incoming[:, 3, :].reshape(-1)
    valid_flat = is_valid.reshape(-1)
    lanes = 128
    plane_rows = cell_total // lanes
    row_hot = ((safe_cells // lanes)[:, None] == jnp.arange(plane_rows, dtype=jnp.int32)[None, :]).astype(jnp.float32)
    row_hot = row_hot * valid_flat.astype(jnp.float32)[:, None]
    lane_hot = (safe_cells % lanes)[:, None] == jnp.arange(lanes, dtype=jnp.int32)[None, :]

    material_hot = (
        material[None] == jnp.arange(eps_inf.shape[0], dtype=jnp.int32)[:, None, None, None]
    ).astype(jnp.float32)
    eps_cell = jnp.einsum("m,mxyz->xyz", eps_inf, material_hot, precision=highest)
    sigma_cell = jnp.einsum("m,mxyz->xyz", conductivity, material_hot, precision=highest)
    strength_cell = jnp.einsum("pm,mxyz->pxyz", pole_strength, material_hot, precision=highest)
    decay_cell = jnp.einsum("pm,mxyz->pxyz", pole_decay, material_hot, precision=highest)
    cells = (eps_cell, sigma_cell, strength_cell, decay_cell)

    def sample(e_now):
        picked = jnp.dot(row_hot, e_now[2].reshape(plane_rows, lanes), precision=highest)
        return jnp.sum(jnp.where(lane_hot, picked, 0.0), axis=1)

    def wire_of(values):
        spread = jnp.where(lane_hot, values[:, None], 0.0)
        return jnp.einsum("kr,kl->rl", row_hot, spread, precision=highest).reshape(grid_shape)

    sample_0 = sample(e_field)
    h_field = magnetic_update(e_field, h_field)
    curr_cell_1 = recv_curr + recv_gain * (sample_0 - recv_drop)
    e_field, polarization = electric_update(e_field, h_field, polarization, wire_of(curr_cell_1), cells)
    sample_1 = sample(e_field)

    returned = from_slots(exchange(jnp.stack([sample_0, sample_1]).reshape(2, n_gy, capacity).transpose(1, 0, 2)))
    seg_sample_0, seg_sample_1 = returned[0], returned[1]
    curr_1 = curr_0 + gain_row * (seg_sample_0 - drop_0)
    curr_prev = jnp.concatenate([single_zero, curr_1[:-1]])
    volt_1 = volt_0 - cap_row * (curr_1 - curr_prev)
    drop_1 = jnp.concatenate([volt_1[1:], single_zero]) - volt_1
    curr_2 = curr_1 + gain_row * (seg_sample_1 - drop_1)
    curr_prev = jnp.concatenate([single_zero, curr_2[:-1]])
    volt_2 = volt_1 - cap_row * (curr_2 - curr_prev)

    h_field = magnetic_update(e_field, h_field)
    recv_curr_2 = exchange(to_slots(curr_2[None], [0.0])).transpose(1, 0, 2).reshape(-1)
    e_field, polarization = electric_update(e_field, h_field, polarization, wire_of(recv_curr_2), cells)
    return (e_field, h_field, polarization, curr_2[None], volt_2[None])


def solution(mesh):
    return jax.shard_map(
        on_device,
        mesh=mesh,
        in_specs=(
            P(None, "gx", "gy", None),
            P(None, "gx", "gy", None),
            P(None, None, "gx", "gy", None),
            P("gx", "gy", None),
            P(),
            P(),
            P(),
            P(),
            P("gx", "gy", None),
            P("gx", "gy"),
            P("gx", "gy"),
            P("gx", "gy"),
            P("gx", "gy"),
            P("gx", "gy"),
        ),
        out_specs=(
            P(None, "gx", "gy", None),
            P(None, "gx", "gy", None),
            P(None, None, "gx", "gy", None),
            P("gx", "gy"),
            P("gx", "gy"),
        ),
        check_vma=False,
    )
```

```python
import jax
import jax.numpy as jnp
from jax import lax
from jax.sharding import PartitionSpec as P

STEPS = 2


TIME_STEP = 0.5


def passed_along(value, axis, steps):
    count = lax.axis_size(axis)
    first, last = (max(0, -steps), min(count, count - steps))
    return lax.ppermute(value, axis, [(source, source + steps) for source in range(first, last)])


def next_vertical(field):
    return jnp.concatenate([field[..., 1:], jnp.zeros_like(field[..., :1])], axis=-1)


def prev_vertical(field):
    return jnp.concatenate([jnp.zeros_like(field[..., :1]), field[..., :-1]], axis=-1)


def electric_rims(e_field):
    face_x = passed_along(e_field[1:3, :1], "gx", -1)
    plus_x = jnp.concatenate([e_field[1:3, 1:], face_x], axis=1)
    face_y = passed_along(e_field[0::2, :, :1], "gy", -1)
    plus_y = jnp.concatenate([e_field[0::2, :, 1:], face_y], axis=2)
    return (plus_x, plus_y)


def magnetic_rims(h_field):
    face_x = passed_along(h_field[1:3, -1:], "gx", 1)
    minus_x = jnp.concatenate([face_x, h_field[1:3, :-1]], axis=1)
    face_y = passed_along(h_field[0::2, :, -1:], "gy", 1)
    minus_y = jnp.concatenate([face_y, h_field[0::2, :, :-1]], axis=2)
    return (minus_x, minus_y)


def magnetic_update(e_field, h_field):
    plus_x, plus_y = electric_rims(e_field)
    elec_x, elec_y, elec_z = (e_field[0], e_field[1], e_field[2])
    magn_x = h_field[0] - TIME_STEP * (plus_y[1] - elec_z - (next_vertical(elec_y) - elec_y))
    magn_y = h_field[1] - TIME_STEP * (next_vertical(elec_x) - elec_x - (plus_x[1] - elec_z))
    magn_z = h_field[2] - TIME_STEP * (plus_x[0] - elec_y - (plus_y[0] - elec_x))
    return jnp.stack([magn_x, magn_y, magn_z])


def electric_base(e_field, h_field, polarization, cells):
    eps_cell, sigma_cell, strength_cell, decay_cell = cells
    magn_x, magn_y, magn_z = (h_field[0], h_field[1], h_field[2])
    minus_x, minus_y = magnetic_rims(h_field)
    curl_x = magn_z - minus_y[1] - (magn_y - prev_vertical(magn_y))
    curl_y = magn_x - prev_vertical(magn_x) - (magn_z - minus_x[1])
    curl_z = magn_y - minus_x[0] - (magn_x - minus_y[0])
    curl_all = jnp.stack([curl_x, curl_y, curl_z])
    polar_new = (
        decay_cell[:, None] * polarization
        + (1.0 - decay_cell[:, None]) * strength_cell[:, None] * e_field[None]
    )
    change = jnp.sum(polar_new - polarization, axis=0)
    drive = TIME_STEP * curl_all - TIME_STEP * sigma_cell[None] * e_field - change
    return (drive, polar_new)


def electric_finish(e_field, drive, wire_term, cells):
    drive = drive.at[2].add(-TIME_STEP * wire_term)
    return e_field + drive / cells[0][None]


def on_device(
    e_field,
    h_field,
    polarization,
    material,
    eps_inf,
    conductivity,
    pole_strength,
    pole_decay,
    seg_owner,
    seg_cell,
    current,
    voltage,
    wire_gain,
    wire_cap,
):
    n_gy = lax.axis_size("gy")
    seg_count = seg_owner.shape[1]
    capacity = max(2 * seg_count // n_gy, 16)
    owner_col = seg_owner[0, :, 0]
    cell_ids = seg_cell[0]
    owner_hot = (owner_col[:, None] == jnp.arange(n_gy, dtype=jnp.int32)[None, :]).astype(jnp.int32)
    rank_in = jnp.sum((jnp.cumsum(owner_hot, axis=0) - 1) * owner_hot, axis=1)
    slot_at = owner_col * capacity + rank_in
    grid_shape = material.shape
    cell_total = grid_shape[0] * grid_shape[1] * grid_shape[2]
    single_zero = jnp.zeros((1,), jnp.float32)

    slot_total = n_gy * capacity
    highest = lax.Precision.HIGHEST
    slot_hot = (jnp.arange(slot_total, dtype=jnp.int32)[:, None] == slot_at[None, :]).astype(jnp.float32)
    slot_used = jnp.sum(slot_hot, axis=1)

    def to_slots(rows, fill):
        placed = jnp.einsum("fs,ts->ft", rows, slot_hot, precision=highest)
        buffer = placed + jnp.asarray(fill, jnp.float32)[:, None] * (1.0 - slot_used)[None, :]
        return buffer.reshape(rows.shape[0], n_gy, capacity).transpose(1, 0, 2)

    def exchange(blocks):
        return lax.all_to_all(blocks, "gy", split_axis=0, concat_axis=0, tiled=True)

    def from_slots(blocks):
        flat = blocks.transpose(1, 0, 2).reshape(blocks.shape[1], slot_total)
        return jnp.einsum("ft,ts->fs", flat, slot_hot, precision=highest)

    gain_row = wire_gain[0]
    cap_row = wire_cap[0]
    volt_0 = voltage[0]
    curr_0 = current[0]
    drop_0 = jnp.concatenate([volt_0[1:], single_zero]) - volt_0
    outgoing = to_slots(jnp.stack([cell_ids.astype(jnp.float32), curr_0, gain_row, drop_0]), [-1.0, 0.0, 0.0, 0.0])
    incoming = exchange(outgoing)

    material_hot = (
        material[None] == jnp.arange(eps_inf.shape[0], dtype=jnp.int32)[:, None, None, None]
    ).astype(jnp.float32)
    eps_cell = jnp.einsum("m,mxyz->xyz", eps_inf, material_hot, precision=highest)
    sigma_cell = jnp.einsum("m,mxyz->xyz", conductivity, material_hot, precision=highest)
    strength_cell = jnp.einsum("pm,mxyz->pxyz", pole_strength, material_hot, precision=highest)
    decay_cell = jnp.einsum("pm,mxyz->pxyz", pole_decay, material_hot, precision=highest)
    cells = (eps_cell, sigma_cell, strength_cell, decay_cell)

    h_field = magnetic_update(e_field, h_field)
    drive, polar_next = electric_base(e_field, h_field, polarization, cells)
    incoming, drive = lax.optimization_barrier((incoming, drive))

    recv_cells = incoming[:, 0, :].astype(jnp.int32)
    is_valid = recv_cells >= 0
    safe_cells = jnp.where(is_valid, recv_cells, 0).reshape(-1)
    recv_curr = incoming[:, 1, :].reshape(-1)
    recv_gain = incoming[:, 2, :].reshape(-1)
    recv_drop = incoming[:, 3, :].reshape(-1)
    valid_flat = is_valid.reshape(-1)
    lanes = 128
    plane_rows = cell_total // lanes
    row_hot = ((safe_cells // lanes)[:, None] == jnp.arange(plane_rows, dtype=jnp.int32)[None, :]).astype(jnp.float32)
    row_hot = row_hot * valid_flat.astype(jnp.float32)[:, None]
    lane_hot = (safe_cells % lanes)[:, None] == jnp.arange(lanes, dtype=jnp.int32)[None, :]

    def sample(e_now):
        picked = jnp.dot(row_hot, e_now[2].reshape(plane_rows, lanes), precision=highest)
        return jnp.sum(jnp.where(lane_hot, picked, 0.0), axis=1)

    def wire_of(values):
        spread = jnp.where(lane_hot, values[:, None], 0.0)
        return jnp.einsum("kr,kl->rl", row_hot, spread, precision=highest).reshape(grid_shape)

    sample_0 = sample(e_field)
    curr_cell_1 = recv_curr + recv_gain * (sample_0 - recv_drop)
    e_field = electric_finish(e_field, drive, wire_of(curr_cell_1), cells)
    polarization = polar_next
    sample_1 = sample(e_field)

    returned = exchange(jnp.stack([sample_0, sample_1]).reshape(2, n_gy, capacity).transpose(1, 0, 2))
    returned, e_field, h_field, polarization = lax.optimization_barrier((returned, e_field, h_field, polarization))
    returned = from_slots(returned)
    seg_sample_0, seg_sample_1 = returned[0], returned[1]
    curr_1 = curr_0 + gain_row * (seg_sample_0 - drop_0)
    curr_prev = jnp.concatenate([single_zero, curr_1[:-1]])
    volt_1 = volt_0 - cap_row * (curr_1 - curr_prev)
    drop_1 = jnp.concatenate([volt_1[1:], single_zero]) - volt_1
    curr_2 = curr_1 + gain_row * (seg_sample_1 - drop_1)
    curr_prev = jnp.concatenate([single_zero, curr_2[:-1]])
    volt_2 = volt_1 - cap_row * (curr_2 - curr_prev)
    recv_curr_2 = exchange(to_slots(curr_2[None], [0.0]))

    h_field = magnetic_update(e_field, h_field)
    drive, polarization = electric_base(e_field, h_field, polarization, cells)
    recv_curr_2, drive = lax.optimization_barrier((recv_curr_2, drive))
    e_field = electric_finish(e_field, drive, wire_of(recv_curr_2.transpose(1, 0, 2).reshape(-1)), cells)
    return (e_field, h_field, polarization, curr_2[None], volt_2[None])


def solution(mesh):
    return jax.shard_map(
        on_device,
        mesh=mesh,
        in_specs=(
            P(None, "gx", "gy", None),
            P(None, "gx", "gy", None),
            P(None, None, "gx", "gy", None),
            P("gx", "gy", None),
            P(),
            P(),
            P(),
            P(),
            P("gx", "gy", None),
            P("gx", "gy"),
            P("gx", "gy"),
            P("gx", "gy"),
            P("gx", "gy"),
            P("gx", "gy"),
        ),
        out_specs=(
            P(None, "gx", "gy", None),
            P(None, "gx", "gy", None),
            P(None, None, "gx", "gy", None),
            P("gx", "gy"),
            P("gx", "gy"),
        ),
        check_vma=False,
    )
```

```python
import jax
import jax.numpy as jnp
from jax import lax
from jax.sharding import PartitionSpec as P

STEPS = 2


TIME_STEP = 0.5


def passed_along(value, axis, steps):
    count = lax.axis_size(axis)
    first, last = (max(0, -steps), min(count, count - steps))
    return lax.ppermute(value, axis, [(source, source + steps) for source in range(first, last)])


def next_vertical(field):
    return jnp.concatenate([field[..., 1:], jnp.zeros_like(field[..., :1])], axis=-1)


def prev_vertical(field):
    return jnp.concatenate([jnp.zeros_like(field[..., :1]), field[..., :-1]], axis=-1)


def electric_rims(e_field):
    face_x = passed_along(e_field[1:3, :1], "gx", -1)
    plus_x = jnp.concatenate([e_field[1:3, 1:], face_x], axis=1)
    face_y = passed_along(e_field[0::2, :, :1], "gy", -1)
    plus_y = jnp.concatenate([e_field[0::2, :, 1:], face_y], axis=2)
    return (plus_x, plus_y)


def magnetic_rims(h_field):
    face_x = passed_along(h_field[1:3, -1:], "gx", 1)
    minus_x = jnp.concatenate([face_x, h_field[1:3, :-1]], axis=1)
    face_y = passed_along(h_field[0::2, :, -1:], "gy", 1)
    minus_y = jnp.concatenate([face_y, h_field[0::2, :, :-1]], axis=2)
    return (minus_x, minus_y)


def magnetic_update(e_field, h_field):
    plus_x, plus_y = electric_rims(e_field)
    elec_x, elec_y, elec_z = (e_field[0], e_field[1], e_field[2])
    magn_x = h_field[0] - TIME_STEP * (plus_y[1] - elec_z - (next_vertical(elec_y) - elec_y))
    magn_y = h_field[1] - TIME_STEP * (next_vertical(elec_x) - elec_x - (plus_x[1] - elec_z))
    magn_z = h_field[2] - TIME_STEP * (plus_x[0] - elec_y - (plus_y[0] - elec_x))
    return jnp.stack([magn_x, magn_y, magn_z])


def electric_base(e_field, h_field, polarization, cells):
    eps_cell, sigma_cell, strength_cell, decay_cell = cells
    magn_x, magn_y, magn_z = (h_field[0], h_field[1], h_field[2])
    minus_x, minus_y = magnetic_rims(h_field)
    curl_x = magn_z - minus_y[1] - (magn_y - prev_vertical(magn_y))
    curl_y = magn_x - prev_vertical(magn_x) - (magn_z - minus_x[1])
    curl_z = magn_y - minus_x[0] - (magn_x - minus_y[0])
    curl_all = jnp.stack([curl_x, curl_y, curl_z])
    polar_new = (
        decay_cell[:, None] * polarization
        + (1.0 - decay_cell[:, None]) * strength_cell[:, None] * e_field[None]
    )
    change = jnp.sum(polar_new - polarization, axis=0)
    drive = TIME_STEP * curl_all - TIME_STEP * sigma_cell[None] * e_field - change
    return (drive, polar_new)


def electric_finish(e_field, drive, wire_term, cells):
    drive = drive.at[2].add(-TIME_STEP * wire_term)
    return e_field + drive / cells[0][None]


def on_device(
    e_field,
    h_field,
    polarization,
    material,
    eps_inf,
    conductivity,
    pole_strength,
    pole_decay,
    seg_owner,
    seg_cell,
    current,
    voltage,
    wire_gain,
    wire_cap,
):
    n_gy = lax.axis_size("gy")
    seg_count = seg_owner.shape[1]
    capacity = max(2 * seg_count // n_gy, 16)
    owner_col = seg_owner[0, :, 0]
    cell_ids = seg_cell[0]
    owner_hot = (owner_col[:, None] == jnp.arange(n_gy, dtype=jnp.int32)[None, :]).astype(jnp.int32)
    rank_in = jnp.sum((jnp.cumsum(owner_hot, axis=0) - 1) * owner_hot, axis=1)
    slot_at = owner_col * capacity + rank_in
    grid_shape = material.shape
    cell_total = grid_shape[0] * grid_shape[1] * grid_shape[2]
    single_zero = jnp.zeros((1,), jnp.float32)

    slot_total = n_gy * capacity
    highest = lax.Precision.HIGHEST
    slot_hot = (jnp.arange(slot_total, dtype=jnp.int32)[:, None] == slot_at[None, :]).astype(jnp.float32)
    slot_used = jnp.sum(slot_hot, axis=1)

    def to_slots(rows, fill):
        placed = jnp.einsum("fs,ts->ft", rows, slot_hot, precision=highest)
        buffer = placed + jnp.asarray(fill, jnp.float32)[:, None] * (1.0 - slot_used)[None, :]
        return buffer.reshape(rows.shape[0], n_gy, capacity).transpose(1, 0, 2)

    def exchange(blocks):
        return lax.all_to_all(blocks, "gy", split_axis=0, concat_axis=0, tiled=True)

    def from_slots(blocks):
        flat = blocks.transpose(1, 0, 2).reshape(blocks.shape[1], slot_total)
        return jnp.einsum("ft,ts->fs", flat, slot_hot, precision=highest)

    gain_row = wire_gain[0]
    cap_row = wire_cap[0]
    volt_0 = voltage[0]
    curr_0 = current[0]
    drop_0 = jnp.concatenate([volt_0[1:], single_zero]) - volt_0
    outgoing = to_slots(jnp.stack([cell_ids.astype(jnp.float32), curr_0, gain_row, drop_0]), [-1.0, 0.0, 0.0, 0.0])
    incoming = exchange(outgoing)

    material_hot = (
        material[None] == jnp.arange(eps_inf.shape[0], dtype=jnp.int32)[:, None, None, None]
    ).astype(jnp.float32)
    eps_cell = jnp.einsum("m,mxyz->xyz", eps_inf, material_hot, precision=highest)
    sigma_cell = jnp.einsum("m,mxyz->xyz", conductivity, material_hot, precision=highest)
    strength_cell = jnp.einsum("pm,mxyz->pxyz", pole_strength, material_hot, precision=highest)
    decay_cell = jnp.einsum("pm,mxyz->pxyz", pole_decay, material_hot, precision=highest)
    cells = (eps_cell, sigma_cell, strength_cell, decay_cell)

    h_field = magnetic_update(e_field, h_field)
    drive, polar_next = electric_base(e_field, h_field, polarization, cells)
    incoming, drive = lax.optimization_barrier((incoming, drive))

    recv_cells = incoming[:, 0, :].astype(jnp.int32)
    is_valid = recv_cells >= 0
    safe_cells = jnp.where(is_valid, recv_cells, 0).reshape(-1)
    recv_curr = incoming[:, 1, :].reshape(-1)
    recv_gain = incoming[:, 2, :].reshape(-1)
    recv_drop = incoming[:, 3, :].reshape(-1)
    valid_flat = is_valid.reshape(-1)
    lanes = 128
    plane_rows = cell_total // lanes
    row_hot = ((safe_cells // lanes)[:, None] == jnp.arange(plane_rows, dtype=jnp.int32)[None, :]).astype(jnp.float32)
    row_hot = row_hot * valid_flat.astype(jnp.float32)[:, None]
    lane_hot = (safe_cells % lanes)[:, None] == jnp.arange(lanes, dtype=jnp.int32)[None, :]

    def sample(e_now):
        picked = jnp.dot(row_hot, e_now[2].reshape(plane_rows, lanes), precision=highest)
        return jnp.sum(jnp.where(lane_hot, picked, 0.0), axis=1)

    def wire_of(values):
        spread = jnp.where(lane_hot, values[:, None], 0.0)
        return jnp.einsum("kr,kl->rl", row_hot, spread, precision=highest).reshape(grid_shape)

    sample_0 = sample(e_field)
    curr_cell_1 = recv_curr + recv_gain * (sample_0 - recv_drop)
    e_field = electric_finish(e_field, drive, wire_of(curr_cell_1), cells)
    polarization = polar_next
    sample_1 = sample(e_field)

    back = jnp.stack([sample_0, sample_1]).reshape(2, n_gy, capacity).transpose(1, 0, 2)
    back, e_field, h_field, polarization = lax.optimization_barrier((back, e_field, h_field, polarization))
    returned = from_slots(exchange(back))
    seg_sample_0, seg_sample_1 = returned[0], returned[1]
    curr_1 = curr_0 + gain_row * (seg_sample_0 - drop_0)
    curr_prev = jnp.concatenate([single_zero, curr_1[:-1]])
    volt_1 = volt_0 - cap_row * (curr_1 - curr_prev)
    drop_1 = jnp.concatenate([volt_1[1:], single_zero]) - volt_1
    curr_2 = curr_1 + gain_row * (seg_sample_1 - drop_1)
    curr_prev = jnp.concatenate([single_zero, curr_2[:-1]])
    volt_2 = volt_1 - cap_row * (curr_2 - curr_prev)
    h_field = magnetic_update(e_field, h_field)
    recv_curr_2 = exchange(to_slots(curr_2[None], [0.0]))

    drive, polarization = electric_base(e_field, h_field, polarization, cells)
    recv_curr_2, drive = lax.optimization_barrier((recv_curr_2, drive))
    e_field = electric_finish(e_field, drive, wire_of(recv_curr_2.transpose(1, 0, 2).reshape(-1)), cells)
    return (e_field, h_field, polarization, curr_2[None], volt_2[None])


def solution(mesh):
    return jax.shard_map(
        on_device,
        mesh=mesh,
        in_specs=(
            P(None, "gx", "gy", None),
            P(None, "gx", "gy", None),
            P(None, None, "gx", "gy", None),
            P("gx", "gy", None),
            P(),
            P(),
            P(),
            P(),
            P("gx", "gy", None),
            P("gx", "gy"),
            P("gx", "gy"),
            P("gx", "gy"),
            P("gx", "gy"),
            P("gx", "gy"),
        ),
        out_specs=(
            P(None, "gx", "gy", None),
            P(None, "gx", "gy", None),
            P(None, None, "gx", "gy", None),
            P("gx", "gy"),
            P("gx", "gy"),
        ),
        check_vma=False,
    )
```

```python
import jax
import jax.numpy as jnp
from jax import lax
from jax.sharding import PartitionSpec as P

STEPS = 2


TIME_STEP = 0.5


def passed_along(value, axis, steps):
    count = lax.axis_size(axis)
    first, last = (max(0, -steps), min(count, count - steps))
    return lax.ppermute(value, axis, [(source, source + steps) for source in range(first, last)])


def next_vertical(field):
    return jnp.concatenate([field[..., 1:], jnp.zeros_like(field[..., :1])], axis=-1)


def prev_vertical(field):
    return jnp.concatenate([jnp.zeros_like(field[..., :1]), field[..., :-1]], axis=-1)


def electric_rims(e_field):
    face_x = passed_along(e_field[1:3, :1], "gx", -1)
    plus_x = jnp.concatenate([e_field[1:3, 1:], face_x], axis=1)
    face_y = passed_along(e_field[0::2, :, :1], "gy", -1)
    plus_y = jnp.concatenate([e_field[0::2, :, 1:], face_y], axis=2)
    return (plus_x, plus_y)


def magnetic_rims(h_field):
    face_x = passed_along(h_field[1:3, -1:], "gx", 1)
    minus_x = jnp.concatenate([face_x, h_field[1:3, :-1]], axis=1)
    face_y = passed_along(h_field[0::2, :, -1:], "gy", 1)
    minus_y = jnp.concatenate([face_y, h_field[0::2, :, :-1]], axis=2)
    return (minus_x, minus_y)


def magnetic_update(e_field, h_field):
    plus_x, plus_y = electric_rims(e_field)
    elec_x, elec_y, elec_z = (e_field[0], e_field[1], e_field[2])
    magn_x = h_field[0] - TIME_STEP * (plus_y[1] - elec_z - (next_vertical(elec_y) - elec_y))
    magn_y = h_field[1] - TIME_STEP * (next_vertical(elec_x) - elec_x - (plus_x[1] - elec_z))
    magn_z = h_field[2] - TIME_STEP * (plus_x[0] - elec_y - (plus_y[0] - elec_x))
    return jnp.stack([magn_x, magn_y, magn_z])


def electric_base(e_field, h_field, polarization, cells):
    eps_cell, sigma_cell, strength_cell, decay_cell = cells
    magn_x, magn_y, magn_z = (h_field[0], h_field[1], h_field[2])
    minus_x, minus_y = magnetic_rims(h_field)
    curl_x = magn_z - minus_y[1] - (magn_y - prev_vertical(magn_y))
    curl_y = magn_x - prev_vertical(magn_x) - (magn_z - minus_x[1])
    curl_z = magn_y - minus_x[0] - (magn_x - minus_y[0])
    curl_all = jnp.stack([curl_x, curl_y, curl_z])
    polar_new = (
        decay_cell[:, None] * polarization
        + (1.0 - decay_cell[:, None]) * strength_cell[:, None] * e_field[None]
    )
    change = jnp.sum(polar_new - polarization, axis=0)
    drive = TIME_STEP * curl_all - TIME_STEP * sigma_cell[None] * e_field - change
    return (drive, polar_new)


def electric_finish(e_field, drive, wire_term, cells):
    drive = drive.at[2].add(-TIME_STEP * wire_term)
    return e_field + drive / cells[0][None]


def on_device(
    e_field,
    h_field,
    polarization,
    material,
    eps_inf,
    conductivity,
    pole_strength,
    pole_decay,
    seg_owner,
    seg_cell,
    current,
    voltage,
    wire_gain,
    wire_cap,
):
    n_gy = lax.axis_size("gy")
    seg_count = seg_owner.shape[1]
    capacity = max(2 * seg_count // n_gy, 16)
    owner_col = seg_owner[0, :, 0]
    cell_ids = seg_cell[0]
    owner_hot = (owner_col[:, None] == jnp.arange(n_gy, dtype=jnp.int32)[None, :]).astype(jnp.int32)
    rank_in = jnp.sum((jnp.cumsum(owner_hot, axis=0) - 1) * owner_hot, axis=1)
    slot_at = owner_col * capacity + rank_in
    grid_shape = material.shape
    cell_total = grid_shape[0] * grid_shape[1] * grid_shape[2]
    single_zero = jnp.zeros((1,), jnp.float32)

    slot_total = n_gy * capacity
    highest = lax.Precision.HIGHEST
    slot_hot = (jnp.arange(slot_total, dtype=jnp.int32)[:, None] == slot_at[None, :]).astype(jnp.float32)
    slot_used = jnp.sum(slot_hot, axis=1)

    def to_slots(rows, fill):
        placed = jnp.einsum("fs,ts->ft", rows, slot_hot, precision=highest)
        buffer = placed + jnp.asarray(fill, jnp.float32)[:, None] * (1.0 - slot_used)[None, :]
        return buffer.reshape(rows.shape[0], n_gy, capacity).transpose(1, 0, 2)

    def exchange(blocks):
        return lax.all_to_all(blocks, "gy", split_axis=0, concat_axis=0, tiled=True)

    def from_slots(blocks):
        flat = blocks.transpose(1, 0, 2).reshape(blocks.shape[1], slot_total)
        return jnp.einsum("ft,ts->fs", flat, slot_hot, precision=highest)

    gain_row = wire_gain[0]
    cap_row = wire_cap[0]
    volt_0 = voltage[0]
    curr_0 = current[0]
    drop_0 = jnp.concatenate([volt_0[1:], single_zero]) - volt_0
    outgoing = to_slots(jnp.stack([cell_ids.astype(jnp.float32), curr_0, gain_row, drop_0]), [-1.0, 0.0, 0.0, 0.0])
    incoming = exchange(outgoing)

    material_hot = (
        material[None] == jnp.arange(eps_inf.shape[0], dtype=jnp.int32)[:, None, None, None]
    ).astype(jnp.float32)
    eps_cell = jnp.einsum("m,mxyz->xyz", eps_inf, material_hot, precision=highest)
    sigma_cell = jnp.einsum("m,mxyz->xyz", conductivity, material_hot, precision=highest)
    strength_cell = jnp.einsum("pm,mxyz->pxyz", pole_strength, material_hot, precision=highest)
    decay_cell = jnp.einsum("pm,mxyz->pxyz", pole_decay, material_hot, precision=highest)
    cells = (eps_cell, sigma_cell, strength_cell, decay_cell)

    h_field = magnetic_update(e_field, h_field)
    drive, polar_next = electric_base(e_field, h_field, polarization, cells)
    incoming, drive = lax.optimization_barrier((incoming, drive))

    recv_cells = incoming[:, 0, :].astype(jnp.int32)
    is_valid = recv_cells >= 0
    safe_cells = jnp.where(is_valid, recv_cells, 0).reshape(-1)
    recv_curr = incoming[:, 1, :].reshape(-1)
    recv_gain = incoming[:, 2, :].reshape(-1)
    recv_drop = incoming[:, 3, :].reshape(-1)
    valid_flat = is_valid.reshape(-1)
    lanes = 128
    plane_rows = cell_total // lanes
    row_hot = ((safe_cells // lanes)[:, None] == jnp.arange(plane_rows, dtype=jnp.int32)[None, :]).astype(jnp.float32)
    row_hot = row_hot * valid_flat.astype(jnp.float32)[:, None]
    lane_hot = (safe_cells % lanes)[:, None] == jnp.arange(lanes, dtype=jnp.int32)[None, :]

    def sample(e_now):
        picked = jnp.dot(row_hot, e_now[2].reshape(plane_rows, lanes), precision=highest)
        return jnp.sum(jnp.where(lane_hot, picked, 0.0), axis=1)

    def wire_of(values):
        spread = jnp.where(lane_hot, values[:, None], 0.0)
        return jnp.einsum("kr,kl->rl", row_hot, spread, precision=highest).reshape(grid_shape)

    def plane(field):
        return field.reshape(plane_rows, lanes)

    def pick(planes):
        picked = jnp.dot(row_hot, jnp.concatenate(planes, axis=1), precision=highest)
        return [jnp.sum(jnp.where(lane_hot, picked[:, i * lanes:(i + 1) * lanes], 0.0), axis=1) for i in range(len(planes))]

    sample_0, drive_at, eps_at = pick([plane(e_field[2]), plane(drive[2]), plane(eps_cell)])
    curr_cell_1 = recv_curr + recv_gain * (sample_0 - recv_drop)
    wire_plane = jnp.einsum("kr,kl->rl", row_hot, jnp.where(lane_hot, curr_cell_1[:, None], 0.0), precision=highest)
    (wire_at,) = pick([wire_plane])
    sample_1 = jnp.where(valid_flat, sample_0 + (drive_at + -TIME_STEP * wire_at) / eps_at, 0.0)
    polarization = polar_next

    back = jnp.stack([sample_0, sample_1]).reshape(2, n_gy, capacity).transpose(1, 0, 2)
    back, drive, wire_plane, h_field, polarization = lax.optimization_barrier((back, drive, wire_plane, h_field, polarization))
    e_field = electric_finish(e_field, drive, wire_plane.reshape(grid_shape), cells)
    returned = from_slots(exchange(back))
    seg_sample_0, seg_sample_1 = returned[0], returned[1]
    curr_1 = curr_0 + gain_row * (seg_sample_0 - drop_0)
    curr_prev = jnp.concatenate([single_zero, curr_1[:-1]])
    volt_1 = volt_0 - cap_row * (curr_1 - curr_prev)
    drop_1 = jnp.concatenate([volt_1[1:], single_zero]) - volt_1
    curr_2 = curr_1 + gain_row * (seg_sample_1 - drop_1)
    curr_prev = jnp.concatenate([single_zero, curr_2[:-1]])
    volt_2 = volt_1 - cap_row * (curr_2 - curr_prev)
    h_field = magnetic_update(e_field, h_field)
    recv_curr_2 = exchange(to_slots(curr_2[None], [0.0]))

    drive, polarization = electric_base(e_field, h_field, polarization, cells)
    recv_curr_2, drive = lax.optimization_barrier((recv_curr_2, drive))
    e_field = electric_finish(e_field, drive, wire_of(recv_curr_2.transpose(1, 0, 2).reshape(-1)), cells)
    return (e_field, h_field, polarization, curr_2[None], volt_2[None])


def solution(mesh):
    return jax.shard_map(
        on_device,
        mesh=mesh,
        in_specs=(
            P(None, "gx", "gy", None),
            P(None, "gx", "gy", None),
            P(None, None, "gx", "gy", None),
            P("gx", "gy", None),
            P(),
            P(),
            P(),
            P(),
            P("gx", "gy", None),
            P("gx", "gy"),
            P("gx", "gy"),
            P("gx", "gy"),
            P("gx", "gy"),
            P("gx", "gy"),
        ),
        out_specs=(
            P(None, "gx", "gy", None),
            P(None, "gx", "gy", None),
            P(None, None, "gx", "gy", None),
            P("gx", "gy"),
            P("gx", "gy"),
        ),
        check_vma=False,
    )
```

```python
import jax
import jax.numpy as jnp
from jax import lax
from jax.sharding import PartitionSpec as P

STEPS = 2


TIME_STEP = 0.5


def passed_along(value, axis, steps):
    count = lax.axis_size(axis)
    first, last = (max(0, -steps), min(count, count - steps))
    return lax.ppermute(value, axis, [(source, source + steps) for source in range(first, last)])


def next_vertical(field):
    return jnp.concatenate([field[..., 1:], jnp.zeros_like(field[..., :1])], axis=-1)


def prev_vertical(field):
    return jnp.concatenate([jnp.zeros_like(field[..., :1]), field[..., :-1]], axis=-1)


def electric_rims(e_field):
    face_x = passed_along(e_field[1:3, :1], "gx", -1)
    plus_x = jnp.concatenate([e_field[1:3, 1:], face_x], axis=1)
    face_y = passed_along(e_field[0::2, :, :1], "gy", -1)
    plus_y = jnp.concatenate([e_field[0::2, :, 1:], face_y], axis=2)
    return (plus_x, plus_y)


def magnetic_rims(h_field):
    face_x = passed_along(h_field[1:3, -1:], "gx", 1)
    minus_x = jnp.concatenate([face_x, h_field[1:3, :-1]], axis=1)
    face_y = passed_along(h_field[0::2, :, -1:], "gy", 1)
    minus_y = jnp.concatenate([face_y, h_field[0::2, :, :-1]], axis=2)
    return (minus_x, minus_y)


def magnetic_update(e_field, h_field):
    plus_x, plus_y = electric_rims(e_field)
    elec_x, elec_y, elec_z = (e_field[0], e_field[1], e_field[2])
    magn_x = h_field[0] - TIME_STEP * (plus_y[1] - elec_z - (next_vertical(elec_y) - elec_y))
    magn_y = h_field[1] - TIME_STEP * (next_vertical(elec_x) - elec_x - (plus_x[1] - elec_z))
    magn_z = h_field[2] - TIME_STEP * (plus_x[0] - elec_y - (plus_y[0] - elec_x))
    return jnp.stack([magn_x, magn_y, magn_z])


def electric_base(e_field, h_field, polarization, cells):
    eps_cell, sigma_cell, strength_cell, decay_cell = cells
    magn_x, magn_y, magn_z = (h_field[0], h_field[1], h_field[2])
    minus_x, minus_y = magnetic_rims(h_field)
    curl_x = magn_z - minus_y[1] - (magn_y - prev_vertical(magn_y))
    curl_y = magn_x - prev_vertical(magn_x) - (magn_z - minus_x[1])
    curl_z = magn_y - minus_x[0] - (magn_x - minus_y[0])
    curl_all = jnp.stack([curl_x, curl_y, curl_z])
    polar_new = (
        decay_cell[:, None] * polarization
        + (1.0 - decay_cell[:, None]) * strength_cell[:, None] * e_field[None]
    )
    change = jnp.sum(polar_new - polarization, axis=0)
    drive = TIME_STEP * curl_all - TIME_STEP * sigma_cell[None] * e_field - change
    return (drive, polar_new)


def electric_finish(e_field, drive, wire_term, cells):
    drive = drive.at[2].add(-TIME_STEP * wire_term)
    return e_field + drive / cells[0][None]


def on_device(
    e_field,
    h_field,
    polarization,
    material,
    eps_inf,
    conductivity,
    pole_strength,
    pole_decay,
    seg_owner,
    seg_cell,
    current,
    voltage,
    wire_gain,
    wire_cap,
):
    n_gy = lax.axis_size("gy")
    seg_count = seg_owner.shape[1]
    capacity = max(2 * seg_count // n_gy, 16)
    owner_col = seg_owner[0, :, 0]
    cell_ids = seg_cell[0]
    owner_hot = (owner_col[:, None] == jnp.arange(n_gy, dtype=jnp.int32)[None, :]).astype(jnp.int32)
    rank_in = jnp.sum((jnp.cumsum(owner_hot, axis=0) - 1) * owner_hot, axis=1)
    slot_at = owner_col * capacity + rank_in
    grid_shape = material.shape
    cell_total = grid_shape[0] * grid_shape[1] * grid_shape[2]
    single_zero = jnp.zeros((1,), jnp.float32)

    slot_total = n_gy * capacity
    highest = lax.Precision.HIGHEST
    slot_hot = (jnp.arange(slot_total, dtype=jnp.int32)[:, None] == slot_at[None, :]).astype(jnp.float32)
    slot_used = jnp.sum(slot_hot, axis=1)

    def to_slots(rows, fill):
        placed = jnp.einsum("fs,ts->ft", rows, slot_hot, precision=highest)
        buffer = placed + jnp.asarray(fill, jnp.float32)[:, None] * (1.0 - slot_used)[None, :]
        return buffer.reshape(rows.shape[0], n_gy, capacity).transpose(1, 0, 2)

    def exchange(blocks):
        return lax.all_to_all(blocks, "gy", split_axis=0, concat_axis=0, tiled=True)

    def from_slots(blocks):
        flat = blocks.transpose(1, 0, 2).reshape(blocks.shape[1], slot_total)
        return jnp.einsum("ft,ts->fs", flat, slot_hot, precision=highest)

    gain_row = wire_gain[0]
    cap_row = wire_cap[0]
    volt_0 = voltage[0]
    curr_0 = current[0]
    drop_0 = jnp.concatenate([volt_0[1:], single_zero]) - volt_0
    outgoing = to_slots(jnp.stack([cell_ids.astype(jnp.float32), curr_0, gain_row, drop_0]), [-1.0, 0.0, 0.0, 0.0])
    h_field = magnetic_update(e_field, h_field)
    outgoing, h_field = lax.optimization_barrier((outgoing, h_field))
    incoming = exchange(outgoing)

    material_hot = (
        material[None] == jnp.arange(eps_inf.shape[0], dtype=jnp.int32)[:, None, None, None]
    ).astype(jnp.float32)
    eps_cell = jnp.einsum("m,mxyz->xyz", eps_inf, material_hot, precision=highest)
    sigma_cell = jnp.einsum("m,mxyz->xyz", conductivity, material_hot, precision=highest)
    strength_cell = jnp.einsum("pm,mxyz->pxyz", pole_strength, material_hot, precision=highest)
    decay_cell = jnp.einsum("pm,mxyz->pxyz", pole_decay, material_hot, precision=highest)
    cells = (eps_cell, sigma_cell, strength_cell, decay_cell)

    drive, polar_next = electric_base(e_field, h_field, polarization, cells)
    incoming, drive = lax.optimization_barrier((incoming, drive))

    recv_cells = incoming[:, 0, :].astype(jnp.int32)
    is_valid = recv_cells >= 0
    safe_cells = jnp.where(is_valid, recv_cells, 0).reshape(-1)
    recv_curr = incoming[:, 1, :].reshape(-1)
    recv_gain = incoming[:, 2, :].reshape(-1)
    recv_drop = incoming[:, 3, :].reshape(-1)
    valid_flat = is_valid.reshape(-1)
    lanes = 128
    plane_rows = cell_total // lanes
    row_hot = ((safe_cells // lanes)[:, None] == jnp.arange(plane_rows, dtype=jnp.int32)[None, :]).astype(jnp.float32)
    row_hot = row_hot * valid_flat.astype(jnp.float32)[:, None]
    lane_hot = (safe_cells % lanes)[:, None] == jnp.arange(lanes, dtype=jnp.int32)[None, :]

    def sample(e_now):
        picked = jnp.dot(row_hot, e_now[2].reshape(plane_rows, lanes), precision=highest)
        return jnp.sum(jnp.where(lane_hot, picked, 0.0), axis=1)

    def wire_of(values):
        spread = jnp.where(lane_hot, values[:, None], 0.0)
        return jnp.einsum("kr,kl->rl", row_hot, spread, precision=highest).reshape(grid_shape)

    sample_0 = sample(e_field)
    curr_cell_1 = recv_curr + recv_gain * (sample_0 - recv_drop)
    e_field = electric_finish(e_field, drive, wire_of(curr_cell_1), cells)
    polarization = polar_next
    sample_1 = sample(e_field)

    back = jnp.stack([sample_0, sample_1]).reshape(2, n_gy, capacity).transpose(1, 0, 2)
    back, e_field, h_field, polarization = lax.optimization_barrier((back, e_field, h_field, polarization))
    returned = from_slots(exchange(back))
    seg_sample_0, seg_sample_1 = returned[0], returned[1]
    curr_1 = curr_0 + gain_row * (seg_sample_0 - drop_0)
    curr_prev = jnp.concatenate([single_zero, curr_1[:-1]])
    volt_1 = volt_0 - cap_row * (curr_1 - curr_prev)
    drop_1 = jnp.concatenate([volt_1[1:], single_zero]) - volt_1
    curr_2 = curr_1 + gain_row * (seg_sample_1 - drop_1)
    curr_prev = jnp.concatenate([single_zero, curr_2[:-1]])
    volt_2 = volt_1 - cap_row * (curr_2 - curr_prev)
    h_field = magnetic_update(e_field, h_field)
    recv_curr_2 = exchange(to_slots(curr_2[None], [0.0]))

    drive, polarization = electric_base(e_field, h_field, polarization, cells)
    recv_curr_2, drive = lax.optimization_barrier((recv_curr_2, drive))
    e_field = electric_finish(e_field, drive, wire_of(recv_curr_2.transpose(1, 0, 2).reshape(-1)), cells)
    return (e_field, h_field, polarization, curr_2[None], volt_2[None])


def solution(mesh):
    return jax.shard_map(
        on_device,
        mesh=mesh,
        in_specs=(
            P(None, "gx", "gy", None),
            P(None, "gx", "gy", None),
            P(None, None, "gx", "gy", None),
            P("gx", "gy", None),
            P(),
            P(),
            P(),
            P(),
            P("gx", "gy", None),
            P("gx", "gy"),
            P("gx", "gy"),
            P("gx", "gy"),
            P("gx", "gy"),
            P("gx", "gy"),
        ),
        out_specs=(
            P(None, "gx", "gy", None),
            P(None, "gx", "gy", None),
            P(None, None, "gx", "gy", None),
            P("gx", "gy"),
            P("gx", "gy"),
        ),
        check_vma=False,
    )
```

```python
import jax
import jax.numpy as jnp
from jax import lax
from jax.sharding import PartitionSpec as P

STEPS = 2


TIME_STEP = 0.5


def passed_along(value, axis, steps):
    count = lax.axis_size(axis)
    first, last = (max(0, -steps), min(count, count - steps))
    return lax.ppermute(value, axis, [(source, source + steps) for source in range(first, last)])


def next_vertical(field):
    return jnp.concatenate([field[..., 1:], jnp.zeros_like(field[..., :1])], axis=-1)


def prev_vertical(field):
    return jnp.concatenate([jnp.zeros_like(field[..., :1]), field[..., :-1]], axis=-1)


def electric_rims(e_field):
    face_x = passed_along(e_field[1:3, :1], "gx", -1)
    plus_x = jnp.concatenate([e_field[1:3, 1:], face_x], axis=1)
    face_y = passed_along(e_field[0::2, :, :1], "gy", -1)
    plus_y = jnp.concatenate([e_field[0::2, :, 1:], face_y], axis=2)
    return (plus_x, plus_y)


def magnetic_rims(h_field):
    face_x = passed_along(h_field[1:3, -1:], "gx", 1)
    minus_x = jnp.concatenate([face_x, h_field[1:3, :-1]], axis=1)
    face_y = passed_along(h_field[0::2, :, -1:], "gy", 1)
    minus_y = jnp.concatenate([face_y, h_field[0::2, :, :-1]], axis=2)
    return (minus_x, minus_y)


def magnetic_update(e_field, h_field):
    plus_x, plus_y = electric_rims(e_field)
    elec_x, elec_y, elec_z = (e_field[0], e_field[1], e_field[2])
    magn_x = h_field[0] - TIME_STEP * (plus_y[1] - elec_z - (next_vertical(elec_y) - elec_y))
    magn_y = h_field[1] - TIME_STEP * (next_vertical(elec_x) - elec_x - (plus_x[1] - elec_z))
    magn_z = h_field[2] - TIME_STEP * (plus_x[0] - elec_y - (plus_y[0] - elec_x))
    return jnp.stack([magn_x, magn_y, magn_z])


def electric_base(e_field, h_field, polarization, cells):
    eps_cell, sigma_cell, strength_cell, decay_cell = cells
    magn_x, magn_y, magn_z = (h_field[0], h_field[1], h_field[2])
    minus_x, minus_y = magnetic_rims(h_field)
    curl_x = magn_z - minus_y[1] - (magn_y - prev_vertical(magn_y))
    curl_y = magn_x - prev_vertical(magn_x) - (magn_z - minus_x[1])
    curl_z = magn_y - minus_x[0] - (magn_x - minus_y[0])
    curl_all = jnp.stack([curl_x, curl_y, curl_z])
    polar_new = (
        decay_cell[:, None] * polarization
        + (1.0 - decay_cell[:, None]) * strength_cell[:, None] * e_field[None]
    )
    change = jnp.sum(polar_new - polarization, axis=0)
    drive = TIME_STEP * curl_all - TIME_STEP * sigma_cell[None] * e_field - change
    return (drive, polar_new)


def electric_finish(e_field, drive, wire_term, cells):
    drive = drive.at[2].add(-TIME_STEP * wire_term)
    return e_field + drive / cells[0][None]


def split_parts(values):
    high = lax.reduce_precision(values, exponent_bits=8, mantissa_bits=7)
    rest = values - high
    middle = lax.reduce_precision(rest, exponent_bits=8, mantissa_bits=7)
    low = rest - middle
    return [part.astype(jnp.bfloat16) for part in (high, middle, low)]


def hot_dot(spec, hot, values):
    parts = [jnp.einsum(spec, hot, part, preferred_element_type=jnp.float32) for part in split_parts(values)]
    return (parts[0] + parts[1]) + parts[2]


def on_device(
    e_field,
    h_field,
    polarization,
    material,
    eps_inf,
    conductivity,
    pole_strength,
    pole_decay,
    seg_owner,
    seg_cell,
    current,
    voltage,
    wire_gain,
    wire_cap,
):
    n_gy = lax.axis_size("gy")
    seg_count = seg_owner.shape[1]
    capacity = max(2 * seg_count // n_gy, 16)
    owner_col = seg_owner[0, :, 0]
    cell_ids = seg_cell[0]
    owner_hot = (owner_col[:, None] == jnp.arange(n_gy, dtype=jnp.int32)[None, :]).astype(jnp.int32)
    rank_in = jnp.sum((jnp.cumsum(owner_hot, axis=0) - 1) * owner_hot, axis=1)
    slot_at = owner_col * capacity + rank_in
    grid_shape = material.shape
    cell_total = grid_shape[0] * grid_shape[1] * grid_shape[2]
    single_zero = jnp.zeros((1,), jnp.float32)

    slot_total = n_gy * capacity
    highest = lax.Precision.HIGHEST
    slot_match = jnp.arange(slot_total, dtype=jnp.int32)[:, None] == slot_at[None, :]
    slot_hot = slot_match.astype(jnp.bfloat16)
    slot_used = jnp.sum(slot_match.astype(jnp.float32), axis=1)

    def to_slots(rows, fill):
        placed = hot_dot("ts,fs->ft", slot_hot, rows)
        buffer = placed + jnp.asarray(fill, jnp.float32)[:, None] * (1.0 - slot_used)[None, :]
        return buffer.reshape(rows.shape[0], n_gy, capacity).transpose(1, 0, 2)

    def exchange(blocks):
        return lax.all_to_all(blocks, "gy", split_axis=0, concat_axis=0, tiled=True)

    def from_slots(blocks):
        flat = blocks.transpose(1, 0, 2).reshape(blocks.shape[1], slot_total)
        return hot_dot("ts,ft->fs", slot_hot, flat)

    gain_row = wire_gain[0]
    cap_row = wire_cap[0]
    volt_0 = voltage[0]
    curr_0 = current[0]
    drop_0 = jnp.concatenate([volt_0[1:], single_zero]) - volt_0
    outgoing = to_slots(jnp.stack([cell_ids.astype(jnp.float32), curr_0, gain_row, drop_0]), [-1.0, 0.0, 0.0, 0.0])
    h_field = magnetic_update(e_field, h_field)
    outgoing, h_field = lax.optimization_barrier((outgoing, h_field))
    incoming = exchange(outgoing)

    material_hot = (
        material[None] == jnp.arange(eps_inf.shape[0], dtype=jnp.int32)[:, None, None, None]
    ).astype(jnp.float32)
    eps_cell = jnp.einsum("m,mxyz->xyz", eps_inf, material_hot, precision=highest)
    sigma_cell = jnp.einsum("m,mxyz->xyz", conductivity, material_hot, precision=highest)
    strength_cell = jnp.einsum("pm,mxyz->pxyz", pole_strength, material_hot, precision=highest)
    decay_cell = jnp.einsum("pm,mxyz->pxyz", pole_decay, material_hot, precision=highest)
    cells = (eps_cell, sigma_cell, strength_cell, decay_cell)

    drive, polar_next = electric_base(e_field, h_field, polarization, cells)
    incoming, drive = lax.optimization_barrier((incoming, drive))

    recv_cells = incoming[:, 0, :].astype(jnp.int32)
    is_valid = recv_cells >= 0
    safe_cells = jnp.where(is_valid, recv_cells, 0).reshape(-1)
    recv_curr = incoming[:, 1, :].reshape(-1)
    recv_gain = incoming[:, 2, :].reshape(-1)
    recv_drop = incoming[:, 3, :].reshape(-1)
    valid_flat = is_valid.reshape(-1)
    lanes = 128
    plane_rows = cell_total // lanes
    row_match = (safe_cells // lanes)[:, None] == jnp.arange(plane_rows, dtype=jnp.int32)[None, :]
    row_hot = (row_match & valid_flat[:, None]).astype(jnp.bfloat16)
    lane_hot = (safe_cells % lanes)[:, None] == jnp.arange(lanes, dtype=jnp.int32)[None, :]

    def sample(e_now):
        picked = hot_dot("kr,rl->kl", row_hot, e_now[2].reshape(plane_rows, lanes))
        return jnp.sum(jnp.where(lane_hot, picked, 0.0), axis=1)

    def wire_of(values):
        spread = jnp.where(lane_hot, values[:, None], 0.0)
        return hot_dot("kr,kl->rl", row_hot, spread).reshape(grid_shape)

    sample_0 = sample(e_field)
    curr_cell_1 = recv_curr + recv_gain * (sample_0 - recv_drop)
    e_field = electric_finish(e_field, drive, wire_of(curr_cell_1), cells)
    polarization = polar_next
    sample_1 = sample(e_field)

    back = jnp.stack([sample_0, sample_1]).reshape(2, n_gy, capacity).transpose(1, 0, 2)
    back, e_field, h_field, polarization = lax.optimization_barrier((back, e_field, h_field, polarization))
    returned = from_slots(exchange(back))
    seg_sample_0, seg_sample_1 = returned[0], returned[1]
    curr_1 = curr_0 + gain_row * (seg_sample_0 - drop_0)
    curr_prev = jnp.concatenate([single_zero, curr_1[:-1]])
    volt_1 = volt_0 - cap_row * (curr_1 - curr_prev)
    drop_1 = jnp.concatenate([volt_1[1:], single_zero]) - volt_1
    curr_2 = curr_1 + gain_row * (seg_sample_1 - drop_1)
    curr_prev = jnp.concatenate([single_zero, curr_2[:-1]])
    volt_2 = volt_1 - cap_row * (curr_2 - curr_prev)
    h_field = magnetic_update(e_field, h_field)
    recv_curr_2 = exchange(to_slots(curr_2[None], [0.0]))

    drive, polarization = electric_base(e_field, h_field, polarization, cells)
    recv_curr_2, drive = lax.optimization_barrier((recv_curr_2, drive))
    e_field = electric_finish(e_field, drive, wire_of(recv_curr_2.transpose(1, 0, 2).reshape(-1)), cells)
    return (e_field, h_field, polarization, curr_2[None], volt_2[None])


def solution(mesh):
    return jax.shard_map(
        on_device,
        mesh=mesh,
        in_specs=(
            P(None, "gx", "gy", None),
            P(None, "gx", "gy", None),
            P(None, None, "gx", "gy", None),
            P("gx", "gy", None),
            P(),
            P(),
            P(),
            P(),
            P("gx", "gy", None),
            P("gx", "gy"),
            P("gx", "gy"),
            P("gx", "gy"),
            P("gx", "gy"),
            P("gx", "gy"),
        ),
        out_specs=(
            P(None, "gx", "gy", None),
            P(None, "gx", "gy", None),
            P(None, None, "gx", "gy", None),
            P("gx", "gy"),
            P("gx", "gy"),
        ),
        check_vma=False,
    )
```

```python
import jax
import jax.numpy as jnp
from jax import lax
from jax.sharding import PartitionSpec as P

STEPS = 2


TIME_STEP = 0.5


def passed_along(value, axis, steps):
    count = lax.axis_size(axis)
    first, last = (max(0, -steps), min(count, count - steps))
    return lax.ppermute(value, axis, [(source, source + steps) for source in range(first, last)])


def next_vertical(field):
    return jnp.concatenate([field[..., 1:], jnp.zeros_like(field[..., :1])], axis=-1)


def prev_vertical(field):
    return jnp.concatenate([jnp.zeros_like(field[..., :1]), field[..., :-1]], axis=-1)


def electric_rims(e_field):
    face_x = passed_along(e_field[1:3, :1], "gx", -1)
    plus_x = jnp.concatenate([e_field[1:3, 1:], face_x], axis=1)
    face_y = passed_along(e_field[0::2, :, :1], "gy", -1)
    plus_y = jnp.concatenate([e_field[0::2, :, 1:], face_y], axis=2)
    return (plus_x, plus_y)


def magnetic_rims(h_field):
    face_x = passed_along(h_field[1:3, -1:], "gx", 1)
    minus_x = jnp.concatenate([face_x, h_field[1:3, :-1]], axis=1)
    face_y = passed_along(h_field[0::2, :, -1:], "gy", 1)
    minus_y = jnp.concatenate([face_y, h_field[0::2, :, :-1]], axis=2)
    return (minus_x, minus_y)


def magnetic_update(e_field, h_field):
    plus_x, plus_y = electric_rims(e_field)
    elec_x, elec_y, elec_z = (e_field[0], e_field[1], e_field[2])
    magn_x = h_field[0] - TIME_STEP * (plus_y[1] - elec_z - (next_vertical(elec_y) - elec_y))
    magn_y = h_field[1] - TIME_STEP * (next_vertical(elec_x) - elec_x - (plus_x[1] - elec_z))
    magn_z = h_field[2] - TIME_STEP * (plus_x[0] - elec_y - (plus_y[0] - elec_x))
    return jnp.stack([magn_x, magn_y, magn_z])


def electric_base(e_field, h_field, polarization, cells, rims=None):
    eps_cell, sigma_cell, strength_cell, decay_cell = cells
    magn_x, magn_y, magn_z = (h_field[0], h_field[1], h_field[2])
    minus_x, minus_y = magnetic_rims(h_field) if rims is None else rims
    curl_x = magn_z - minus_y[1] - (magn_y - prev_vertical(magn_y))
    curl_y = magn_x - prev_vertical(magn_x) - (magn_z - minus_x[1])
    curl_z = magn_y - minus_x[0] - (magn_x - minus_y[0])
    curl_all = jnp.stack([curl_x, curl_y, curl_z])
    polar_new = (
        decay_cell[:, None] * polarization
        + (1.0 - decay_cell[:, None]) * strength_cell[:, None] * e_field[None]
    )
    change = jnp.sum(polar_new - polarization, axis=0)
    drive = TIME_STEP * curl_all - TIME_STEP * sigma_cell[None] * e_field - change
    return (drive, polar_new)


def electric_finish(e_field, drive, wire_term, cells):
    drive = drive.at[2].add(-TIME_STEP * wire_term)
    return e_field + drive / cells[0][None]


def on_device(
    e_field,
    h_field,
    polarization,
    material,
    eps_inf,
    conductivity,
    pole_strength,
    pole_decay,
    seg_owner,
    seg_cell,
    current,
    voltage,
    wire_gain,
    wire_cap,
):
    n_gy = lax.axis_size("gy")
    seg_count = seg_owner.shape[1]
    capacity = max(2 * seg_count // n_gy, 16)
    owner_col = seg_owner[0, :, 0]
    cell_ids = seg_cell[0]
    order = jnp.arange(seg_count, dtype=jnp.int32)
    earlier_same = (owner_col[None, :] == owner_col[:, None]) & (order[None, :] < order[:, None])
    rank_in = jnp.sum(earlier_same.astype(jnp.int32), axis=1)
    slot_at = owner_col * capacity + rank_in
    grid_shape = material.shape
    cell_total = grid_shape[0] * grid_shape[1] * grid_shape[2]
    single_zero = jnp.zeros((1,), jnp.float32)

    slot_total = n_gy * capacity
    highest = lax.Precision.HIGHEST
    slot_hot = (jnp.arange(slot_total, dtype=jnp.int32)[:, None] == slot_at[None, :]).astype(jnp.float32)
    slot_used = jnp.sum(slot_hot, axis=1)

    def to_slots(rows, fill):
        placed = jnp.einsum("fs,ts->ft", rows, slot_hot, precision=highest)
        buffer = placed + jnp.asarray(fill, jnp.float32)[:, None] * (1.0 - slot_used)[None, :]
        return buffer.reshape(rows.shape[0], n_gy, capacity).transpose(1, 0, 2)

    def exchange(blocks):
        return lax.all_to_all(blocks, "gy", split_axis=0, concat_axis=0, tiled=True)

    def from_slots(blocks):
        flat = blocks.transpose(1, 0, 2).reshape(blocks.shape[1], slot_total)
        return jnp.einsum("ft,ts->fs", flat, slot_hot, precision=highest)

    gain_row = wire_gain[0]
    cap_row = wire_cap[0]
    volt_0 = voltage[0]
    curr_0 = current[0]
    drop_0 = jnp.concatenate([volt_0[1:], single_zero]) - volt_0
    outgoing = to_slots(jnp.stack([cell_ids.astype(jnp.float32), curr_0, gain_row, drop_0]), [-1.0, 0.0, 0.0, 0.0])
    h_field = magnetic_update(e_field, h_field)
    outgoing, h_field = lax.optimization_barrier((outgoing, h_field))
    incoming = exchange(outgoing)

    material_hot = (
        material[None] == jnp.arange(eps_inf.shape[0], dtype=jnp.int32)[:, None, None, None]
    ).astype(jnp.float32)
    eps_cell = jnp.einsum("m,mxyz->xyz", eps_inf, material_hot, precision=highest)
    sigma_cell = jnp.einsum("m,mxyz->xyz", conductivity, material_hot, precision=highest)
    strength_cell = jnp.einsum("pm,mxyz->pxyz", pole_strength, material_hot, precision=highest)
    decay_cell = jnp.einsum("pm,mxyz->pxyz", pole_decay, material_hot, precision=highest)
    cells = (eps_cell, sigma_cell, strength_cell, decay_cell)

    drive, polar_next = electric_base(e_field, h_field, polarization, cells)
    incoming, drive = lax.optimization_barrier((incoming, drive))

    recv_cells = incoming[:, 0, :].astype(jnp.int32)
    is_valid = recv_cells >= 0
    safe_cells = jnp.where(is_valid, recv_cells, 0).reshape(-1)
    recv_curr = incoming[:, 1, :].reshape(-1)
    recv_gain = incoming[:, 2, :].reshape(-1)
    recv_drop = incoming[:, 3, :].reshape(-1)
    valid_flat = is_valid.reshape(-1)
    lanes = 128
    plane_rows = cell_total // lanes
    row_hot = ((safe_cells // lanes)[:, None] == jnp.arange(plane_rows, dtype=jnp.int32)[None, :]).astype(jnp.float32)
    row_hot = row_hot * valid_flat.astype(jnp.float32)[:, None]
    lane_hot = (safe_cells % lanes)[:, None] == jnp.arange(lanes, dtype=jnp.int32)[None, :]

    def sample(e_now):
        picked = jnp.dot(row_hot, e_now[2].reshape(plane_rows, lanes), precision=highest)
        return jnp.sum(jnp.where(lane_hot, picked, 0.0), axis=1)

    def wire_of(values):
        spread = jnp.where(lane_hot, values[:, None], 0.0)
        return jnp.einsum("kr,kl->rl", row_hot, spread, precision=highest).reshape(grid_shape)

    sample_0 = sample(e_field)
    curr_cell_1 = recv_curr + recv_gain * (sample_0 - recv_drop)
    e_field = electric_finish(e_field, drive, wire_of(curr_cell_1), cells)
    polarization = polar_next
    sample_1 = sample(e_field)

    back = jnp.stack([sample_0, sample_1]).reshape(2, n_gy, capacity).transpose(1, 0, 2)
    back, e_field, h_field, polarization = lax.optimization_barrier((back, e_field, h_field, polarization))
    returned = exchange(back)
    h_field = magnetic_update(e_field, h_field)
    rims = magnetic_rims(h_field)
    returned, rims = lax.optimization_barrier((returned, rims))
    returned = from_slots(returned)
    seg_sample_0, seg_sample_1 = returned[0], returned[1]
    curr_1 = curr_0 + gain_row * (seg_sample_0 - drop_0)
    curr_prev = jnp.concatenate([single_zero, curr_1[:-1]])
    volt_1 = volt_0 - cap_row * (curr_1 - curr_prev)
    drop_1 = jnp.concatenate([volt_1[1:], single_zero]) - volt_1
    curr_2 = curr_1 + gain_row * (seg_sample_1 - drop_1)
    curr_prev = jnp.concatenate([single_zero, curr_2[:-1]])
    volt_2 = volt_1 - cap_row * (curr_2 - curr_prev)
    recv_curr_2 = exchange(to_slots(curr_2[None], [0.0]))

    drive, polarization = electric_base(e_field, h_field, polarization, cells, rims)
    recv_curr_2, drive = lax.optimization_barrier((recv_curr_2, drive))
    e_field = electric_finish(e_field, drive, wire_of(recv_curr_2.transpose(1, 0, 2).reshape(-1)), cells)
    return (e_field, h_field, polarization, curr_2[None], volt_2[None])


def solution(mesh):
    return jax.shard_map(
        on_device,
        mesh=mesh,
        in_specs=(
            P(None, "gx", "gy", None),
            P(None, "gx", "gy", None),
            P(None, None, "gx", "gy", None),
            P("gx", "gy", None),
            P(),
            P(),
            P(),
            P(),
            P("gx", "gy", None),
            P("gx", "gy"),
            P("gx", "gy"),
            P("gx", "gy"),
            P("gx", "gy"),
            P("gx", "gy"),
        ),
        out_specs=(
            P(None, "gx", "gy", None),
            P(None, "gx", "gy", None),
            P(None, None, "gx", "gy", None),
            P("gx", "gy"),
            P("gx", "gy"),
        ),
        check_vma=False,
    )
```

```python
import jax
import jax.numpy as jnp
from jax import lax
from jax.sharding import PartitionSpec as P

STEPS = 2


TIME_STEP = 0.5


def passed_along(value, axis, steps):
    count = lax.axis_size(axis)
    first, last = (max(0, -steps), min(count, count - steps))
    return lax.ppermute(value, axis, [(source, source + steps) for source in range(first, last)])


def next_vertical(field):
    return jnp.concatenate([field[..., 1:], jnp.zeros_like(field[..., :1])], axis=-1)


def prev_vertical(field):
    return jnp.concatenate([jnp.zeros_like(field[..., :1]), field[..., :-1]], axis=-1)


def electric_rims(e_field):
    face_x = passed_along(e_field[1:3, :1], "gx", -1)
    plus_x = jnp.concatenate([e_field[1:3, 1:], face_x], axis=1)
    face_y = passed_along(e_field[0::2, :, :1], "gy", -1)
    plus_y = jnp.concatenate([e_field[0::2, :, 1:], face_y], axis=2)
    return (plus_x, plus_y)


def magnetic_rims(h_field):
    face_x = passed_along(h_field[1:3, -1:], "gx", 1)
    minus_x = jnp.concatenate([face_x, h_field[1:3, :-1]], axis=1)
    face_y = passed_along(h_field[0::2, :, -1:], "gy", 1)
    minus_y = jnp.concatenate([face_y, h_field[0::2, :, :-1]], axis=2)
    return (minus_x, minus_y)


def magnetic_update(e_field, h_field):
    plus_x, plus_y = electric_rims(e_field)
    elec_x, elec_y, elec_z = (e_field[0], e_field[1], e_field[2])
    magn_x = h_field[0] - TIME_STEP * (plus_y[1] - elec_z - (next_vertical(elec_y) - elec_y))
    magn_y = h_field[1] - TIME_STEP * (next_vertical(elec_x) - elec_x - (plus_x[1] - elec_z))
    magn_z = h_field[2] - TIME_STEP * (plus_x[0] - elec_y - (plus_y[0] - elec_x))
    return jnp.stack([magn_x, magn_y, magn_z])


def electric_base(e_field, h_field, polarization, cells):
    eps_cell, sigma_cell, strength_cell, decay_cell = cells
    magn_x, magn_y, magn_z = (h_field[0], h_field[1], h_field[2])
    minus_x, minus_y = magnetic_rims(h_field)
    curl_x = magn_z - minus_y[1] - (magn_y - prev_vertical(magn_y))
    curl_y = magn_x - prev_vertical(magn_x) - (magn_z - minus_x[1])
    curl_z = magn_y - minus_x[0] - (magn_x - minus_y[0])
    curl_all = jnp.stack([curl_x, curl_y, curl_z])
    polar_new = (
        decay_cell[:, None] * polarization
        + (1.0 - decay_cell[:, None]) * strength_cell[:, None] * e_field[None]
    )
    change = jnp.sum(polar_new - polarization, axis=0)
    drive = TIME_STEP * curl_all - TIME_STEP * sigma_cell[None] * e_field - change
    return (drive, polar_new)


def electric_finish(e_field, drive, wire_term, cells):
    drive = drive.at[2].add(-TIME_STEP * wire_term)
    return e_field + drive / cells[0][None]


def on_device(
    e_field,
    h_field,
    polarization,
    material,
    eps_inf,
    conductivity,
    pole_strength,
    pole_decay,
    seg_owner,
    seg_cell,
    current,
    voltage,
    wire_gain,
    wire_cap,
):
    n_gy = lax.axis_size("gy")
    seg_count = seg_owner.shape[1]
    capacity = max(2 * seg_count // n_gy, 16)
    owner_col = seg_owner[0, :, 0]
    cell_ids = seg_cell[0]
    order = jnp.arange(seg_count, dtype=jnp.int32)
    earlier_same = (owner_col[None, :] == owner_col[:, None]) & (order[None, :] < order[:, None])
    rank_in = jnp.sum(earlier_same.astype(jnp.int32), axis=1)
    slot_at = owner_col * capacity + rank_in
    grid_shape = material.shape
    cell_total = grid_shape[0] * grid_shape[1] * grid_shape[2]
    single_zero = jnp.zeros((1,), jnp.float32)

    slot_total = n_gy * capacity
    highest = lax.Precision.HIGHEST
    slot_hot = (jnp.arange(slot_total, dtype=jnp.int32)[:, None] == slot_at[None, :]).astype(jnp.float32)
    slot_used = jnp.sum(slot_hot, axis=1)

    def to_slots(rows, fill):
        placed = jnp.einsum("fs,ts->ft", rows, slot_hot, precision=highest)
        buffer = placed + jnp.asarray(fill, jnp.float32)[:, None] * (1.0 - slot_used)[None, :]
        return buffer.reshape(rows.shape[0], n_gy, capacity).transpose(1, 0, 2)

    def exchange(blocks):
        return lax.all_to_all(blocks, "gy", split_axis=0, concat_axis=0, tiled=True)

    def from_slots(blocks):
        flat = blocks.transpose(1, 0, 2).reshape(blocks.shape[1], slot_total)
        return jnp.einsum("ft,ts->fs", flat, slot_hot, precision=highest)

    gain_row = wire_gain[0]
    cap_row = wire_cap[0]
    volt_0 = voltage[0]
    curr_0 = current[0]
    drop_0 = jnp.concatenate([volt_0[1:], single_zero]) - volt_0
    outgoing = to_slots(jnp.stack([cell_ids.astype(jnp.float32), curr_0, gain_row, drop_0]), [-1.0, 0.0, 0.0, 0.0])
    h_field = magnetic_update(e_field, h_field)
    outgoing, h_field = lax.optimization_barrier((outgoing, h_field))
    incoming = exchange(outgoing)

    material_hot = (
        material[None] == jnp.arange(eps_inf.shape[0], dtype=jnp.int32)[:, None, None, None]
    ).astype(jnp.float32)
    eps_cell = jnp.einsum("m,mxyz->xyz", eps_inf, material_hot, precision=highest)
    sigma_cell = jnp.einsum("m,mxyz->xyz", conductivity, material_hot, precision=highest)
    strength_cell = jnp.einsum("pm,mxyz->pxyz", pole_strength, material_hot, precision=highest)
    decay_cell = jnp.einsum("pm,mxyz->pxyz", pole_decay, material_hot, precision=highest)
    cells = (eps_cell, sigma_cell, strength_cell, decay_cell)

    drive, polar_next = electric_base(e_field, h_field, polarization, cells)
    incoming, drive = lax.optimization_barrier((incoming, drive))

    recv_cells = incoming[:, 0, :].astype(jnp.int32)
    is_valid = recv_cells >= 0
    safe_cells = jnp.where(is_valid, recv_cells, 0).reshape(-1)
    recv_curr = incoming[:, 1, :].reshape(-1)
    recv_gain = incoming[:, 2, :].reshape(-1)
    recv_drop = incoming[:, 3, :].reshape(-1)
    valid_flat = is_valid.reshape(-1)
    lanes = 128
    plane_rows = cell_total // lanes
    row_hot = ((safe_cells // lanes)[:, None] == jnp.arange(plane_rows, dtype=jnp.int32)[None, :]).astype(jnp.float32)
    row_hot = row_hot * valid_flat.astype(jnp.float32)[:, None]
    lane_hot = (safe_cells % lanes)[:, None] == jnp.arange(lanes, dtype=jnp.int32)[None, :]

    def sample(e_now):
        picked = jnp.dot(row_hot, e_now[2].reshape(plane_rows, lanes), precision=highest)
        return jnp.sum(jnp.where(lane_hot, picked, 0.0), axis=1)

    def wire_of(values):
        spread = jnp.where(lane_hot, values[:, None], 0.0)
        return jnp.einsum("kr,kl->rl", row_hot, spread, precision=highest).reshape(grid_shape)

    sample_0 = sample(e_field)
    curr_cell_1 = recv_curr + recv_gain * (sample_0 - recv_drop)
    e_field = electric_finish(e_field, drive, wire_of(curr_cell_1), cells)
    polarization = polar_next
    sample_1 = sample(e_field)

    back = jnp.stack([sample_0, sample_1]).reshape(2, n_gy, capacity).transpose(1, 0, 2)
    back, e_field, h_field, polarization = lax.optimization_barrier((back, e_field, h_field, polarization))
    returned = from_slots(exchange(back))
    seg_sample_0, seg_sample_1 = returned[0], returned[1]
    curr_1 = curr_0 + gain_row * (seg_sample_0 - drop_0)
    curr_prev = jnp.concatenate([single_zero, curr_1[:-1]])
    volt_1 = volt_0 - cap_row * (curr_1 - curr_prev)
    drop_1 = jnp.concatenate([volt_1[1:], single_zero]) - volt_1
    curr_2 = curr_1 + gain_row * (seg_sample_1 - drop_1)
    curr_prev = jnp.concatenate([single_zero, curr_2[:-1]])
    volt_2 = volt_1 - cap_row * (curr_2 - curr_prev)
    h_field = magnetic_update(e_field, h_field)
    recv_curr_2 = exchange(to_slots(curr_2[None], [0.0]))

    drive, polarization = electric_base(e_field, h_field, polarization, cells)
    recv_curr_2, drive = lax.optimization_barrier((recv_curr_2, drive))
    e_field = electric_finish(e_field, drive, wire_of(recv_curr_2.transpose(1, 0, 2).reshape(-1)), cells)
    return (e_field, h_field, polarization, curr_2[None], volt_2[None])


def solution(mesh):
    return jax.shard_map(
        on_device,
        mesh=mesh,
        in_specs=(
            P(None, "gx", "gy", None),
            P(None, "gx", "gy", None),
            P(None, None, "gx", "gy", None),
            P("gx", "gy", None),
            P(),
            P(),
            P(),
            P(),
            P("gx", "gy", None),
            P("gx", "gy"),
            P("gx", "gy"),
            P("gx", "gy"),
            P("gx", "gy"),
            P("gx", "gy"),
        ),
        out_specs=(
            P(None, "gx", "gy", None),
            P(None, "gx", "gy", None),
            P(None, None, "gx", "gy", None),
            P("gx", "gy"),
            P("gx", "gy"),
        ),
        check_vma=False,
    )
```

```python
import jax
import jax.numpy as jnp
from jax import lax
from jax.sharding import PartitionSpec as P

STEPS = 2


TIME_STEP = 0.5


def passed_along(value, axis, steps):
    count = lax.axis_size(axis)
    first, last = (max(0, -steps), min(count, count - steps))
    return lax.ppermute(value, axis, [(source, source + steps) for source in range(first, last)])


def next_vertical(field):
    return jnp.concatenate([field[..., 1:], jnp.zeros_like(field[..., :1])], axis=-1)


def prev_vertical(field):
    return jnp.concatenate([jnp.zeros_like(field[..., :1]), field[..., :-1]], axis=-1)


def electric_rims(e_field):
    face_x = passed_along(e_field[1:3, :1], "gx", -1)
    plus_x = jnp.concatenate([e_field[1:3, 1:], face_x], axis=1)
    face_y = passed_along(e_field[0::2, :, :1], "gy", -1)
    plus_y = jnp.concatenate([e_field[0::2, :, 1:], face_y], axis=2)
    return (plus_x, plus_y)


def magnetic_rims(h_field):
    face_x = passed_along(h_field[1:3, -1:], "gx", 1)
    minus_x = jnp.concatenate([face_x, h_field[1:3, :-1]], axis=1)
    face_y = passed_along(h_field[0::2, :, -1:], "gy", 1)
    minus_y = jnp.concatenate([face_y, h_field[0::2, :, :-1]], axis=2)
    return (minus_x, minus_y)


def magnetic_update(e_field, h_field):
    plus_x, plus_y = electric_rims(e_field)
    elec_x, elec_y, elec_z = (e_field[0], e_field[1], e_field[2])
    magn_x = h_field[0] - TIME_STEP * (plus_y[1] - elec_z - (next_vertical(elec_y) - elec_y))
    magn_y = h_field[1] - TIME_STEP * (next_vertical(elec_x) - elec_x - (plus_x[1] - elec_z))
    magn_z = h_field[2] - TIME_STEP * (plus_x[0] - elec_y - (plus_y[0] - elec_x))
    return jnp.stack([magn_x, magn_y, magn_z])


def electric_base(e_field, h_field, polarization, cells):
    eps_cell, sigma_cell, strength_cell, decay_cell = cells
    magn_x, magn_y, magn_z = (h_field[0], h_field[1], h_field[2])
    minus_x, minus_y = magnetic_rims(h_field)
    curl_x = magn_z - minus_y[1] - (magn_y - prev_vertical(magn_y))
    curl_y = magn_x - prev_vertical(magn_x) - (magn_z - minus_x[1])
    curl_z = magn_y - minus_x[0] - (magn_x - minus_y[0])
    curl_all = jnp.stack([curl_x, curl_y, curl_z])
    polar_new = (
        decay_cell[:, None] * polarization
        + (1.0 - decay_cell[:, None]) * strength_cell[:, None] * e_field[None]
    )
    change = jnp.sum(polar_new - polarization, axis=0)
    drive = TIME_STEP * curl_all - TIME_STEP * sigma_cell[None] * e_field - change
    return (drive, polar_new)


def electric_finish(e_field, drive, wire_term, cells):
    drive = drive.at[2].add(-TIME_STEP * wire_term)
    return e_field + drive / cells[0][None]


def on_device(
    e_field,
    h_field,
    polarization,
    material,
    eps_inf,
    conductivity,
    pole_strength,
    pole_decay,
    seg_owner,
    seg_cell,
    current,
    voltage,
    wire_gain,
    wire_cap,
):
    n_gy = lax.axis_size("gy")
    seg_count = seg_owner.shape[1]
    capacity = max(2 * seg_count // n_gy, 16)
    owner_col = seg_owner[0, :, 0]
    cell_ids = seg_cell[0]
    order = jnp.arange(seg_count, dtype=jnp.int32)
    earlier_same = (owner_col[None, :] == owner_col[:, None]) & (order[None, :] < order[:, None])
    rank_in = jnp.sum(earlier_same.astype(jnp.int32), axis=1)
    slot_at = owner_col * capacity + rank_in
    grid_shape = material.shape
    cell_total = grid_shape[0] * grid_shape[1] * grid_shape[2]
    single_zero = jnp.zeros((1,), jnp.float32)

    slot_total = n_gy * capacity
    highest = lax.Precision.HIGHEST
    slot_hot = (jnp.arange(slot_total, dtype=jnp.int32)[:, None] == slot_at[None, :]).astype(jnp.float32)
    slot_used = jnp.sum(slot_hot, axis=1)

    def to_slots(rows, fill):
        placed = jnp.einsum("fs,ts->ft", rows, slot_hot, precision=highest)
        buffer = placed + jnp.asarray(fill, jnp.float32)[:, None] * (1.0 - slot_used)[None, :]
        return buffer.reshape(rows.shape[0], n_gy, capacity).transpose(1, 0, 2)

    def exchange(blocks):
        return lax.all_to_all(blocks, "gy", split_axis=0, concat_axis=0, tiled=True)

    def from_slots(blocks):
        flat = blocks.transpose(1, 0, 2).reshape(blocks.shape[1], slot_total)
        return jnp.einsum("ft,ts->fs", flat, slot_hot, precision=highest)

    gain_row = wire_gain[0]
    cap_row = wire_cap[0]
    volt_0 = voltage[0]
    curr_0 = current[0]
    drop_0 = jnp.concatenate([volt_0[1:], single_zero]) - volt_0
    outgoing = to_slots(jnp.stack([cell_ids.astype(jnp.float32), curr_0, gain_row, drop_0]), [-1.0, 0.0, 0.0, 0.0])
    h_field = magnetic_update(e_field, h_field)
    outgoing, h_field = lax.optimization_barrier((outgoing, h_field))
    incoming = exchange(outgoing)

    material_hot = (
        material[None] == jnp.arange(eps_inf.shape[0], dtype=jnp.int32)[:, None, None, None]
    ).astype(jnp.float32)
    eps_cell = jnp.einsum("m,mxyz->xyz", eps_inf, material_hot, precision=highest)
    sigma_cell = jnp.einsum("m,mxyz->xyz", conductivity, material_hot, precision=highest)
    strength_cell = jnp.einsum("pm,mxyz->pxyz", pole_strength, material_hot, precision=highest)
    decay_cell = jnp.einsum("pm,mxyz->pxyz", pole_decay, material_hot, precision=highest)
    cells = (eps_cell, sigma_cell, strength_cell, decay_cell)

    drive, polar_next = electric_base(e_field, h_field, polarization, cells)
    incoming, drive = lax.optimization_barrier((incoming, drive))

    recv_cells = incoming[:, 0, :].astype(jnp.int32)
    is_valid = recv_cells >= 0
    safe_cells = jnp.where(is_valid, recv_cells, 0)
    recv_curr = incoming[:, 1, :]
    recv_gain = incoming[:, 2, :]
    recv_drop = incoming[:, 3, :]
    lanes = 128
    plane_rows = cell_total // lanes
    row_hot = ((safe_cells // lanes)[:, :, None] == jnp.arange(plane_rows, dtype=jnp.int32)).astype(jnp.float32)
    row_hot = row_hot * is_valid.astype(jnp.float32)[:, :, None]
    lane_hot = (safe_cells % lanes)[:, :, None] == jnp.arange(lanes, dtype=jnp.int32)

    def sample(e_now):
        picked = jnp.einsum("scr,rl->scl", row_hot, e_now[2].reshape(plane_rows, lanes), precision=highest)
        return jnp.sum(jnp.where(lane_hot, picked, 0.0), axis=2)

    def wire_of(values):
        spread = jnp.where(lane_hot, values[:, :, None], 0.0)
        return jnp.einsum("scr,scl->rl", row_hot, spread, precision=highest).reshape(grid_shape)

    sample_0 = sample(e_field)
    curr_cell_1 = recv_curr + recv_gain * (sample_0 - recv_drop)
    e_field = electric_finish(e_field, drive, wire_of(curr_cell_1), cells)
    polarization = polar_next
    sample_1 = sample(e_field)

    back = jnp.stack([sample_0, sample_1], axis=1)
    back, e_field, h_field, polarization = lax.optimization_barrier((back, e_field, h_field, polarization))
    returned = from_slots(exchange(back))
    seg_sample_0, seg_sample_1 = returned[0], returned[1]
    curr_1 = curr_0 + gain_row * (seg_sample_0 - drop_0)
    curr_prev = jnp.concatenate([single_zero, curr_1[:-1]])
    volt_1 = volt_0 - cap_row * (curr_1 - curr_prev)
    drop_1 = jnp.concatenate([volt_1[1:], single_zero]) - volt_1
    curr_2 = curr_1 + gain_row * (seg_sample_1 - drop_1)
    curr_prev = jnp.concatenate([single_zero, curr_2[:-1]])
    volt_2 = volt_1 - cap_row * (curr_2 - curr_prev)
    h_field = magnetic_update(e_field, h_field)
    recv_curr_2 = exchange(to_slots(curr_2[None], [0.0]))

    drive, polarization = electric_base(e_field, h_field, polarization, cells)
    recv_curr_2, drive = lax.optimization_barrier((recv_curr_2, drive))
    e_field = electric_finish(e_field, drive, wire_of(recv_curr_2[:, 0, :]), cells)
    return (e_field, h_field, polarization, curr_2[None], volt_2[None])


def solution(mesh):
    return jax.shard_map(
        on_device,
        mesh=mesh,
        in_specs=(
            P(None, "gx", "gy", None),
            P(None, "gx", "gy", None),
            P(None, None, "gx", "gy", None),
            P("gx", "gy", None),
            P(),
            P(),
            P(),
            P(),
            P("gx", "gy", None),
            P("gx", "gy"),
            P("gx", "gy"),
            P("gx", "gy"),
            P("gx", "gy"),
            P("gx", "gy"),
        ),
        out_specs=(
            P(None, "gx", "gy", None),
            P(None, "gx", "gy", None),
            P(None, None, "gx", "gy", None),
            P("gx", "gy"),
            P("gx", "gy"),
        ),
        check_vma=False,
    )
```

```python
import jax
import jax.numpy as jnp
from jax import lax
from jax.sharding import PartitionSpec as P

STEPS = 2


TIME_STEP = 0.5


def passed_along(value, axis, steps):
    count = lax.axis_size(axis)
    first, last = (max(0, -steps), min(count, count - steps))
    return lax.ppermute(value, axis, [(source, source + steps) for source in range(first, last)])


def next_vertical(field):
    return jnp.concatenate([field[..., 1:], jnp.zeros_like(field[..., :1])], axis=-1)


def prev_vertical(field):
    return jnp.concatenate([jnp.zeros_like(field[..., :1]), field[..., :-1]], axis=-1)


def electric_rims(e_field):
    face_x = passed_along(e_field[1:3, :1], "gx", -1)
    plus_x = jnp.concatenate([e_field[1:3, 1:], face_x], axis=1)
    face_y = passed_along(e_field[0::2, :, :1], "gy", -1)
    plus_y = jnp.concatenate([e_field[0::2, :, 1:], face_y], axis=2)
    return (plus_x, plus_y)


def magnetic_rims(h_field):
    face_x = passed_along(h_field[1:3, -1:], "gx", 1)
    minus_x = jnp.concatenate([face_x, h_field[1:3, :-1]], axis=1)
    face_y = passed_along(h_field[0::2, :, -1:], "gy", 1)
    minus_y = jnp.concatenate([face_y, h_field[0::2, :, :-1]], axis=2)
    return (minus_x, minus_y)


def magnetic_update(e_field, h_field):
    plus_x, plus_y = electric_rims(e_field)
    elec_x, elec_y, elec_z = (e_field[0], e_field[1], e_field[2])
    magn_x = h_field[0] - TIME_STEP * (plus_y[1] - elec_z - (next_vertical(elec_y) - elec_y))
    magn_y = h_field[1] - TIME_STEP * (next_vertical(elec_x) - elec_x - (plus_x[1] - elec_z))
    magn_z = h_field[2] - TIME_STEP * (plus_x[0] - elec_y - (plus_y[0] - elec_x))
    return jnp.stack([magn_x, magn_y, magn_z])


def electric_base(e_field, h_field, polarization, cells):
    eps_cell, sigma_cell, strength_cell, decay_cell = cells
    magn_x, magn_y, magn_z = (h_field[0], h_field[1], h_field[2])
    minus_x, minus_y = magnetic_rims(h_field)
    curl_x = magn_z - minus_y[1] - (magn_y - prev_vertical(magn_y))
    curl_y = magn_x - prev_vertical(magn_x) - (magn_z - minus_x[1])
    curl_z = magn_y - minus_x[0] - (magn_x - minus_y[0])
    curl_all = jnp.stack([curl_x, curl_y, curl_z])
    polar_new = (
        decay_cell[:, None] * polarization
        + (1.0 - decay_cell[:, None]) * strength_cell[:, None] * e_field[None]
    )
    change = jnp.sum(polar_new - polarization, axis=0)
    drive = TIME_STEP * curl_all - TIME_STEP * sigma_cell[None] * e_field - change
    return (drive, polar_new)


def electric_finish(e_field, drive, wire_term, cells):
    drive = drive.at[2].add(-TIME_STEP * wire_term)
    return e_field + drive / cells[0][None]


def on_device(
    e_field,
    h_field,
    polarization,
    material,
    eps_inf,
    conductivity,
    pole_strength,
    pole_decay,
    seg_owner,
    seg_cell,
    current,
    voltage,
    wire_gain,
    wire_cap,
):
    n_gy = lax.axis_size("gy")
    seg_count = seg_owner.shape[1]
    capacity = max(2 * seg_count // n_gy, 16)
    owner_col = seg_owner[0, :, 0]
    cell_ids = seg_cell[0]
    order = jnp.arange(seg_count, dtype=jnp.int32)
    earlier_same = (owner_col[None, :] == owner_col[:, None]) & (order[None, :] < order[:, None])
    rank_in = jnp.sum(earlier_same.astype(jnp.int32), axis=1)
    slot_at = owner_col * capacity + rank_in
    grid_shape = material.shape
    cell_total = grid_shape[0] * grid_shape[1] * grid_shape[2]
    single_zero = jnp.zeros((1,), jnp.float32)

    highest = lax.Precision.HIGHEST
    slot_index = jnp.arange(n_gy, dtype=jnp.int32)[:, None] * capacity + jnp.arange(capacity, dtype=jnp.int32)[None, :]
    slot_match = slot_index[:, :, None] == slot_at[None, None, :]
    slot_hot = slot_match.astype(jnp.float32)
    slot_used = jnp.sum(slot_hot, axis=2)

    def to_slots(rows, fill):
        placed = jnp.einsum("dcs,fs->dfc", slot_hot, rows, precision=highest)
        return placed + jnp.asarray(fill, jnp.float32)[None, :, None] * (1.0 - slot_used)[:, None, :]

    def exchange(blocks):
        return lax.all_to_all(blocks, "gy", split_axis=0, concat_axis=0, tiled=True)

    def from_slots(blocks):
        return jnp.einsum("dfc,dcs->fs", blocks, slot_hot, precision=highest)

    gain_row = wire_gain[0]
    cap_row = wire_cap[0]
    volt_0 = voltage[0]
    curr_0 = current[0]
    drop_0 = jnp.concatenate([volt_0[1:], single_zero]) - volt_0
    outgoing = to_slots(jnp.stack([cell_ids.astype(jnp.float32), curr_0, gain_row, drop_0]), [-1.0, 0.0, 0.0, 0.0])
    h_field = magnetic_update(e_field, h_field)
    outgoing, h_field = lax.optimization_barrier((outgoing, h_field))
    incoming = exchange(outgoing)

    material_hot = (
        material[None] == jnp.arange(eps_inf.shape[0], dtype=jnp.int32)[:, None, None, None]
    ).astype(jnp.float32)
    eps_cell = jnp.einsum("m,mxyz->xyz", eps_inf, material_hot, precision=highest)
    sigma_cell = jnp.einsum("m,mxyz->xyz", conductivity, material_hot, precision=highest)
    strength_cell = jnp.einsum("pm,mxyz->pxyz", pole_strength, material_hot, precision=highest)
    decay_cell = jnp.einsum("pm,mxyz->pxyz", pole_decay, material_hot, precision=highest)
    cells = (eps_cell, sigma_cell, strength_cell, decay_cell)

    drive, polar_next = electric_base(e_field, h_field, polarization, cells)
    incoming, drive = lax.optimization_barrier((incoming, drive))

    recv_cells = incoming[:, 0, :].astype(jnp.int32)
    is_valid = recv_cells >= 0
    safe_cells = jnp.where(is_valid, recv_cells, 0)
    recv_curr = incoming[:, 1, :]
    recv_gain = incoming[:, 2, :]
    recv_drop = incoming[:, 3, :]
    lanes = 128
    plane_rows = cell_total // lanes
    row_hot = ((safe_cells // lanes)[:, :, None] == jnp.arange(plane_rows, dtype=jnp.int32)).astype(jnp.float32)
    row_hot = row_hot * is_valid.astype(jnp.float32)[:, :, None]
    lane_hot = (safe_cells % lanes)[:, :, None] == jnp.arange(lanes, dtype=jnp.int32)

    def sample(e_now):
        picked = jnp.einsum("scr,rl->scl", row_hot, e_now[2].reshape(plane_rows, lanes), precision=highest)
        return jnp.sum(jnp.where(lane_hot, picked, 0.0), axis=2)

    def wire_of(values):
        spread = jnp.where(lane_hot, values[:, :, None], 0.0)
        return jnp.einsum("scr,scl->rl", row_hot, spread, precision=highest).reshape(grid_shape)

    sample_0 = sample(e_field)
    curr_cell_1 = recv_curr + recv_gain * (sample_0 - recv_drop)
    e_field = electric_finish(e_field, drive, wire_of(curr_cell_1), cells)
    polarization = polar_next
    sample_1 = sample(e_field)

    back = jnp.stack([sample_0, sample_1], axis=1)
    back, e_field, h_field, polarization = lax.optimization_barrier((back, e_field, h_field, polarization))
    returned = from_slots(exchange(back))
    seg_sample_0, seg_sample_1 = returned[0], returned[1]
    curr_1 = curr_0 + gain_row * (seg_sample_0 - drop_0)
    curr_prev = jnp.concatenate([single_zero, curr_1[:-1]])
    volt_1 = volt_0 - cap_row * (curr_1 - curr_prev)
    drop_1 = jnp.concatenate([volt_1[1:], single_zero]) - volt_1
    curr_2 = curr_1 + gain_row * (seg_sample_1 - drop_1)
    curr_prev = jnp.concatenate([single_zero, curr_2[:-1]])
    volt_2 = volt_1 - cap_row * (curr_2 - curr_prev)
    h_field = magnetic_update(e_field, h_field)
    recv_curr_2 = exchange(to_slots(curr_2[None], [0.0]))

    drive, polarization = electric_base(e_field, h_field, polarization, cells)
    recv_curr_2, drive = lax.optimization_barrier((recv_curr_2, drive))
    e_field = electric_finish(e_field, drive, wire_of(recv_curr_2[:, 0, :]), cells)
    return (e_field, h_field, polarization, curr_2[None], volt_2[None])


def solution(mesh):
    return jax.shard_map(
        on_device,
        mesh=mesh,
        in_specs=(
            P(None, "gx", "gy", None),
            P(None, "gx", "gy", None),
            P(None, None, "gx", "gy", None),
            P("gx", "gy", None),
            P(),
            P(),
            P(),
            P(),
            P("gx", "gy", None),
            P("gx", "gy"),
            P("gx", "gy"),
            P("gx", "gy"),
            P("gx", "gy"),
            P("gx", "gy"),
        ),
        out_specs=(
            P(None, "gx", "gy", None),
            P(None, "gx", "gy", None),
            P(None, None, "gx", "gy", None),
            P("gx", "gy"),
            P("gx", "gy"),
        ),
        check_vma=False,
    )
```

```python
import jax
import jax.numpy as jnp
from jax import lax
from jax.sharding import PartitionSpec as P

STEPS = 2


TIME_STEP = 0.5


def passed_along(value, axis, steps):
    count = lax.axis_size(axis)
    first, last = (max(0, -steps), min(count, count - steps))
    return lax.ppermute(value, axis, [(source, source + steps) for source in range(first, last)])


def next_vertical(field):
    return jnp.concatenate([field[..., 1:], jnp.zeros_like(field[..., :1])], axis=-1)


def prev_vertical(field):
    return jnp.concatenate([jnp.zeros_like(field[..., :1]), field[..., :-1]], axis=-1)


def electric_rims(e_field):
    face_x = passed_along(e_field[1:3, :1], "gx", -1)
    plus_x = jnp.concatenate([e_field[1:3, 1:], face_x], axis=1)
    face_y = passed_along(e_field[0::2, :, :1], "gy", -1)
    plus_y = jnp.concatenate([e_field[0::2, :, 1:], face_y], axis=2)
    return (plus_x, plus_y)


def magnetic_rims(h_field):
    face_x = passed_along(h_field[1:3, -1:], "gx", 1)
    minus_x = jnp.concatenate([face_x, h_field[1:3, :-1]], axis=1)
    face_y = passed_along(h_field[0::2, :, -1:], "gy", 1)
    minus_y = jnp.concatenate([face_y, h_field[0::2, :, :-1]], axis=2)
    return (minus_x, minus_y)


def magnetic_update(e_field, h_field):
    plus_x, plus_y = electric_rims(e_field)
    elec_x, elec_y, elec_z = (e_field[0], e_field[1], e_field[2])
    magn_x = h_field[0] - TIME_STEP * (plus_y[1] - elec_z - (next_vertical(elec_y) - elec_y))
    magn_y = h_field[1] - TIME_STEP * (next_vertical(elec_x) - elec_x - (plus_x[1] - elec_z))
    magn_z = h_field[2] - TIME_STEP * (plus_x[0] - elec_y - (plus_y[0] - elec_x))
    return jnp.stack([magn_x, magn_y, magn_z])


def electric_base(e_field, h_field, polarization, cells):
    eps_cell, sigma_cell, strength_cell, decay_cell = cells
    magn_x, magn_y, magn_z = (h_field[0], h_field[1], h_field[2])
    minus_x, minus_y = magnetic_rims(h_field)
    curl_x = magn_z - minus_y[1] - (magn_y - prev_vertical(magn_y))
    curl_y = magn_x - prev_vertical(magn_x) - (magn_z - minus_x[1])
    curl_z = magn_y - minus_x[0] - (magn_x - minus_y[0])
    curl_all = jnp.stack([curl_x, curl_y, curl_z])
    polar_new = (
        decay_cell[:, None] * polarization
        + (1.0 - decay_cell[:, None]) * strength_cell[:, None] * e_field[None]
    )
    change = jnp.sum(polar_new - polarization, axis=0)
    drive = TIME_STEP * curl_all - TIME_STEP * sigma_cell[None] * e_field - change
    return (drive, polar_new)


def electric_finish(e_field, drive, wire_term, cells):
    drive = drive.at[2].add(-TIME_STEP * wire_term)
    return e_field + drive / cells[0][None]


def on_device(
    e_field,
    h_field,
    polarization,
    material,
    eps_inf,
    conductivity,
    pole_strength,
    pole_decay,
    seg_owner,
    seg_cell,
    current,
    voltage,
    wire_gain,
    wire_cap,
):
    n_gy = lax.axis_size("gy")
    seg_count = seg_owner.shape[1]
    capacity = max(2 * seg_count // n_gy, 16)
    owner_col = seg_owner[0, :, 0]
    cell_ids = seg_cell[0]
    order = jnp.arange(seg_count, dtype=jnp.int32)
    earlier_same = (owner_col[None, :] == owner_col[:, None]) & (order[None, :] < order[:, None])
    rank_in = jnp.sum(earlier_same.astype(jnp.int32), axis=1)
    slot_at = owner_col * capacity + rank_in
    grid_shape = material.shape
    cell_total = grid_shape[0] * grid_shape[1] * grid_shape[2]
    single_zero = jnp.zeros((1,), jnp.float32)

    slot_total = n_gy * capacity
    highest = lax.Precision.HIGHEST
    slot_hot = (jnp.arange(slot_total, dtype=jnp.int32)[:, None] == slot_at[None, :]).astype(jnp.float32)
    slot_used = jnp.sum(slot_hot, axis=1)

    def to_slots(rows, fill):
        placed = jnp.einsum("fs,ts->ft", rows, slot_hot, precision=highest)
        buffer = placed + jnp.asarray(fill, jnp.float32)[:, None] * (1.0 - slot_used)[None, :]
        return buffer.reshape(rows.shape[0], n_gy, capacity).transpose(1, 0, 2)

    def exchange(blocks):
        return lax.all_to_all(blocks, "gy", split_axis=0, concat_axis=0, tiled=True)

    def from_slots(blocks):
        flat = blocks.transpose(1, 0, 2).reshape(blocks.shape[1], slot_total)
        return jnp.einsum("ft,ts->fs", flat, slot_hot, precision=highest)

    gain_row = wire_gain[0]
    cap_row = wire_cap[0]
    volt_0 = voltage[0]
    curr_0 = current[0]
    drop_0 = jnp.concatenate([volt_0[1:], single_zero]) - volt_0
    outgoing = to_slots(jnp.stack([cell_ids.astype(jnp.float32), curr_0, gain_row, drop_0]), [-1.0, 0.0, 0.0, 0.0])
    h_field = magnetic_update(e_field, h_field)
    outgoing, h_field = lax.optimization_barrier((outgoing, h_field))
    incoming = exchange(outgoing)

    def per_cell(table):
        picked = jnp.broadcast_to(table[..., 0][..., None, None, None], table.shape[:-1] + grid_shape)
        for index in range(1, table.shape[-1]):
            picked = jnp.where(material == index, table[..., index][..., None, None, None], picked)
        return picked

    eps_cell = per_cell(eps_inf)
    sigma_cell = per_cell(conductivity)
    strength_cell = per_cell(pole_strength)
    decay_cell = per_cell(pole_decay)
    cells = (eps_cell, sigma_cell, strength_cell, decay_cell)

    drive, polar_next = electric_base(e_field, h_field, polarization, cells)
    incoming, drive = lax.optimization_barrier((incoming, drive))

    recv_cells = incoming[:, 0, :].astype(jnp.int32)
    is_valid = recv_cells >= 0
    safe_cells = jnp.where(is_valid, recv_cells, 0)
    recv_curr = incoming[:, 1, :]
    recv_gain = incoming[:, 2, :]
    recv_drop = incoming[:, 3, :]
    lanes = 128
    plane_rows = cell_total // lanes
    row_hot = ((safe_cells // lanes)[:, :, None] == jnp.arange(plane_rows, dtype=jnp.int32)).astype(jnp.float32)
    row_hot = row_hot * is_valid.astype(jnp.float32)[:, :, None]
    lane_hot = (safe_cells % lanes)[:, :, None] == jnp.arange(lanes, dtype=jnp.int32)

    def sample(e_now):
        picked = jnp.einsum("scr,rl->scl", row_hot, e_now[2].reshape(plane_rows, lanes), precision=highest)
        return jnp.sum(jnp.where(lane_hot, picked, 0.0), axis=2)

    def wire_of(values):
        spread = jnp.where(lane_hot, values[:, :, None], 0.0)
        return jnp.einsum("scr,scl->rl", row_hot, spread, precision=highest).reshape(grid_shape)

    sample_0 = sample(e_field)
    curr_cell_1 = recv_curr + recv_gain * (sample_0 - recv_drop)
    e_field = electric_finish(e_field, drive, wire_of(curr_cell_1), cells)
    polarization = polar_next
    sample_1 = sample(e_field)

    back = jnp.stack([sample_0, sample_1], axis=1)
    back, e_field, h_field, polarization = lax.optimization_barrier((back, e_field, h_field, polarization))
    returned = from_slots(exchange(back))
    seg_sample_0, seg_sample_1 = returned[0], returned[1]
    curr_1 = curr_0 + gain_row * (seg_sample_0 - drop_0)
    curr_prev = jnp.concatenate([single_zero, curr_1[:-1]])
    volt_1 = volt_0 - cap_row * (curr_1 - curr_prev)
    drop_1 = jnp.concatenate([volt_1[1:], single_zero]) - volt_1
    curr_2 = curr_1 + gain_row * (seg_sample_1 - drop_1)
    curr_prev = jnp.concatenate([single_zero, curr_2[:-1]])
    volt_2 = volt_1 - cap_row * (curr_2 - curr_prev)
    h_field = magnetic_update(e_field, h_field)
    recv_curr_2 = exchange(to_slots(curr_2[None], [0.0]))

    drive, polarization = electric_base(e_field, h_field, polarization, cells)
    recv_curr_2, drive = lax.optimization_barrier((recv_curr_2, drive))
    e_field = electric_finish(e_field, drive, wire_of(recv_curr_2[:, 0, :]), cells)
    return (e_field, h_field, polarization, curr_2[None], volt_2[None])


def solution(mesh):
    return jax.shard_map(
        on_device,
        mesh=mesh,
        in_specs=(
            P(None, "gx", "gy", None),
            P(None, "gx", "gy", None),
            P(None, None, "gx", "gy", None),
            P("gx", "gy", None),
            P(),
            P(),
            P(),
            P(),
            P("gx", "gy", None),
            P("gx", "gy"),
            P("gx", "gy"),
            P("gx", "gy"),
            P("gx", "gy"),
            P("gx", "gy"),
        ),
        out_specs=(
            P(None, "gx", "gy", None),
            P(None, "gx", "gy", None),
            P(None, None, "gx", "gy", None),
            P("gx", "gy"),
            P("gx", "gy"),
        ),
        check_vma=False,
    )
```

```python
import jax
import jax.numpy as jnp
from jax import lax
from jax.sharding import PartitionSpec as P

STEPS = 2


TIME_STEP = 0.5


def passed_along(value, axis, steps):
    count = lax.axis_size(axis)
    first, last = (max(0, -steps), min(count, count - steps))
    return lax.ppermute(value, axis, [(source, source + steps) for source in range(first, last)])


def next_vertical(field):
    return jnp.concatenate([field[..., 1:], jnp.zeros_like(field[..., :1])], axis=-1)


def prev_vertical(field):
    return jnp.concatenate([jnp.zeros_like(field[..., :1]), field[..., :-1]], axis=-1)


def electric_rims(e_field):
    face_x = passed_along(e_field[1:3, :1], "gx", -1)
    plus_x = jnp.concatenate([e_field[1:3, 1:], face_x], axis=1)
    face_y = passed_along(e_field[0::2, :, :1], "gy", -1)
    plus_y = jnp.concatenate([e_field[0::2, :, 1:], face_y], axis=2)
    return (plus_x, plus_y)


def magnetic_rims(h_field):
    face_x = passed_along(h_field[1:3, -1:], "gx", 1)
    minus_x = jnp.concatenate([face_x, h_field[1:3, :-1]], axis=1)
    face_y = passed_along(h_field[0::2, :, -1:], "gy", 1)
    minus_y = jnp.concatenate([face_y, h_field[0::2, :, :-1]], axis=2)
    return (minus_x, minus_y)


def magnetic_update(e_field, h_field):
    plus_x, plus_y = electric_rims(e_field)
    elec_x, elec_y, elec_z = (e_field[0], e_field[1], e_field[2])
    magn_x = h_field[0] - TIME_STEP * (plus_y[1] - elec_z - (next_vertical(elec_y) - elec_y))
    magn_y = h_field[1] - TIME_STEP * (next_vertical(elec_x) - elec_x - (plus_x[1] - elec_z))
    magn_z = h_field[2] - TIME_STEP * (plus_x[0] - elec_y - (plus_y[0] - elec_x))
    return jnp.stack([magn_x, magn_y, magn_z])


def electric_base(e_field, h_field, polarization, cells):
    eps_cell, sigma_cell, strength_cell, decay_cell = cells
    magn_x, magn_y, magn_z = (h_field[0], h_field[1], h_field[2])
    minus_x, minus_y = magnetic_rims(h_field)
    curl_x = magn_z - minus_y[1] - (magn_y - prev_vertical(magn_y))
    curl_y = magn_x - prev_vertical(magn_x) - (magn_z - minus_x[1])
    curl_z = magn_y - minus_x[0] - (magn_x - minus_y[0])
    curl_all = jnp.stack([curl_x, curl_y, curl_z])
    polar_new = (
        decay_cell[:, None] * polarization
        + (1.0 - decay_cell[:, None]) * strength_cell[:, None] * e_field[None]
    )
    change = jnp.sum(polar_new - polarization, axis=0)
    drive = TIME_STEP * curl_all - TIME_STEP * sigma_cell[None] * e_field - change
    return (drive, polar_new)


def electric_finish(e_field, drive, wire_term, cells):
    drive = drive.at[2].add(-TIME_STEP * wire_term)
    return e_field + drive / cells[0][None]


def on_device(
    e_field,
    h_field,
    polarization,
    material,
    eps_inf,
    conductivity,
    pole_strength,
    pole_decay,
    seg_owner,
    seg_cell,
    current,
    voltage,
    wire_gain,
    wire_cap,
):
    n_gy = lax.axis_size("gy")
    seg_count = seg_owner.shape[1]
    capacity = max(2 * seg_count // n_gy, 16)
    owner_col = seg_owner[0, :, 0]
    cell_ids = seg_cell[0]
    order = jnp.arange(seg_count, dtype=jnp.int32)
    earlier_same = (owner_col[None, :] == owner_col[:, None]) & (order[None, :] < order[:, None])
    rank_in = jnp.sum(earlier_same.astype(jnp.int32), axis=1)
    slot_at = owner_col * capacity + rank_in
    grid_shape = material.shape
    cell_total = grid_shape[0] * grid_shape[1] * grid_shape[2]
    single_zero = jnp.zeros((1,), jnp.float32)

    slot_total = n_gy * capacity
    highest = lax.Precision.HIGHEST
    slot_hot = (jnp.arange(slot_total, dtype=jnp.int32)[:, None] == slot_at[None, :]).astype(jnp.float32)
    slot_used = jnp.sum(slot_hot, axis=1)

    def to_slots(rows, fill):
        placed = jnp.einsum("fs,ts->ft", rows, slot_hot, precision=highest)
        buffer = placed + jnp.asarray(fill, jnp.float32)[:, None] * (1.0 - slot_used)[None, :]
        return buffer.reshape(rows.shape[0], n_gy, capacity).transpose(1, 0, 2)

    def exchange(blocks):
        return lax.all_to_all(blocks, "gy", split_axis=0, concat_axis=0, tiled=True)

    def from_slots(blocks):
        flat = blocks.transpose(1, 0, 2).reshape(blocks.shape[1], slot_total)
        return jnp.einsum("ft,ts->fs", flat, slot_hot, precision=highest)

    gain_row = wire_gain[0]
    cap_row = wire_cap[0]
    volt_0 = voltage[0]
    curr_0 = current[0]
    drop_0 = jnp.concatenate([volt_0[1:], single_zero]) - volt_0
    outgoing = to_slots(jnp.stack([cell_ids.astype(jnp.float32), curr_0, gain_row, drop_0]), [-1.0, 0.0, 0.0, 0.0])
    h_field = magnetic_update(e_field, h_field)
    outgoing, h_field = lax.optimization_barrier((outgoing, h_field))
    incoming = exchange(outgoing)

    material_hot = (
        material[None] == jnp.arange(eps_inf.shape[0], dtype=jnp.int32)[:, None, None, None]
    ).astype(jnp.float32)
    eps_cell = jnp.einsum("m,mxyz->xyz", eps_inf, material_hot, precision=highest)
    sigma_cell = jnp.einsum("m,mxyz->xyz", conductivity, material_hot, precision=highest)
    strength_cell = jnp.einsum("pm,mxyz->pxyz", pole_strength, material_hot, precision=highest)
    decay_cell = jnp.einsum("pm,mxyz->pxyz", pole_decay, material_hot, precision=highest)
    cells = (eps_cell, sigma_cell, strength_cell, decay_cell)

    drive, polar_next = electric_base(e_field, h_field, polarization, cells)
    incoming, drive = lax.optimization_barrier((incoming, drive))

    recv_cells = incoming[:, 0, :].astype(jnp.int32)
    is_valid = recv_cells >= 0
    safe_cells = jnp.where(is_valid, recv_cells, 0)
    recv_curr = incoming[:, 1, :]
    recv_gain = incoming[:, 2, :]
    recv_drop = incoming[:, 3, :]
    lanes = 128
    plane_rows = cell_total // lanes
    row_hot = ((safe_cells // lanes)[:, :, None] == jnp.arange(plane_rows, dtype=jnp.int32)).astype(jnp.float32)
    row_hot = row_hot * is_valid.astype(jnp.float32)[:, :, None]
    lane_hot = (safe_cells % lanes)[:, :, None] == jnp.arange(lanes, dtype=jnp.int32)

    def sample(e_now):
        picked = jnp.einsum("scr,rl->scl", row_hot, e_now[2].reshape(plane_rows, lanes), precision=highest)
        return jnp.sum(jnp.where(lane_hot, picked, 0.0), axis=2)

    def wire_of(values):
        spread = jnp.where(lane_hot, values[:, :, None], 0.0)
        return jnp.einsum("scr,scl->rl", row_hot, spread, precision=highest).reshape(grid_shape)

    sample_0 = sample(e_field)
    curr_cell_1 = recv_curr + recv_gain * (sample_0 - recv_drop)
    spread_1 = jnp.where(lane_hot, curr_cell_1[:, :, None], 0.0)
    wire_plane = jnp.einsum("scr,scl->rl", row_hot, spread_1, precision=highest)
    ez_plane = e_field[2].reshape(plane_rows, lanes) + (
        drive[2].reshape(plane_rows, lanes) + -TIME_STEP * wire_plane
    ) / eps_cell.reshape(plane_rows, lanes)
    picked = jnp.einsum("scr,rl->scl", row_hot, ez_plane, precision=highest)
    sample_1 = jnp.sum(jnp.where(lane_hot, picked, 0.0), axis=2)
    polarization = polar_next

    back = jnp.stack([sample_0, sample_1], axis=1)
    back, drive, wire_plane, h_field, polarization = lax.optimization_barrier((back, drive, wire_plane, h_field, polarization))
    e_field = electric_finish(e_field, drive, wire_plane.reshape(grid_shape), cells)
    returned = from_slots(exchange(back))
    seg_sample_0, seg_sample_1 = returned[0], returned[1]
    curr_1 = curr_0 + gain_row * (seg_sample_0 - drop_0)
    curr_prev = jnp.concatenate([single_zero, curr_1[:-1]])
    volt_1 = volt_0 - cap_row * (curr_1 - curr_prev)
    drop_1 = jnp.concatenate([volt_1[1:], single_zero]) - volt_1
    curr_2 = curr_1 + gain_row * (seg_sample_1 - drop_1)
    curr_prev = jnp.concatenate([single_zero, curr_2[:-1]])
    volt_2 = volt_1 - cap_row * (curr_2 - curr_prev)
    h_field = magnetic_update(e_field, h_field)
    recv_curr_2 = exchange(to_slots(curr_2[None], [0.0]))

    drive, polarization = electric_base(e_field, h_field, polarization, cells)
    recv_curr_2, drive = lax.optimization_barrier((recv_curr_2, drive))
    e_field = electric_finish(e_field, drive, wire_of(recv_curr_2[:, 0, :]), cells)
    return (e_field, h_field, polarization, curr_2[None], volt_2[None])


def solution(mesh):
    return jax.shard_map(
        on_device,
        mesh=mesh,
        in_specs=(
            P(None, "gx", "gy", None),
            P(None, "gx", "gy", None),
            P(None, None, "gx", "gy", None),
            P("gx", "gy", None),
            P(),
            P(),
            P(),
            P(),
            P("gx", "gy", None),
            P("gx", "gy"),
            P("gx", "gy"),
            P("gx", "gy"),
            P("gx", "gy"),
            P("gx", "gy"),
        ),
        out_specs=(
            P(None, "gx", "gy", None),
            P(None, "gx", "gy", None),
            P(None, None, "gx", "gy", None),
            P("gx", "gy"),
            P("gx", "gy"),
        ),
        check_vma=False,
    )
```

```python
import jax
import jax.numpy as jnp
from jax import lax
from jax.sharding import PartitionSpec as P

STEPS = 2


TIME_STEP = 0.5


def passed_along(value, axis, steps):
    count = lax.axis_size(axis)
    first, last = (max(0, -steps), min(count, count - steps))
    return lax.ppermute(value, axis, [(source, source + steps) for source in range(first, last)])


def next_vertical(field):
    return jnp.concatenate([field[..., 1:], jnp.zeros_like(field[..., :1])], axis=-1)


def prev_vertical(field):
    return jnp.concatenate([jnp.zeros_like(field[..., :1]), field[..., :-1]], axis=-1)


def electric_rims(e_field):
    face_x = passed_along(e_field[1:3, :1], "gx", -1)
    plus_x = jnp.concatenate([e_field[1:3, 1:], face_x], axis=1)
    face_y = passed_along(e_field[0::2, :, :1], "gy", -1)
    plus_y = jnp.concatenate([e_field[0::2, :, 1:], face_y], axis=2)
    return (plus_x, plus_y)


def magnetic_rims(h_field):
    face_x = passed_along(h_field[1:3, -1:], "gx", 1)
    minus_x = jnp.concatenate([face_x, h_field[1:3, :-1]], axis=1)
    face_y = passed_along(h_field[0::2, :, -1:], "gy", 1)
    minus_y = jnp.concatenate([face_y, h_field[0::2, :, :-1]], axis=2)
    return (minus_x, minus_y)


def magnetic_update(e_field, h_field):
    plus_x, plus_y = electric_rims(e_field)
    elec_x, elec_y, elec_z = (e_field[0], e_field[1], e_field[2])
    magn_x = h_field[0] - TIME_STEP * (plus_y[1] - elec_z - (next_vertical(elec_y) - elec_y))
    magn_y = h_field[1] - TIME_STEP * (next_vertical(elec_x) - elec_x - (plus_x[1] - elec_z))
    magn_z = h_field[2] - TIME_STEP * (plus_x[0] - elec_y - (plus_y[0] - elec_x))
    return jnp.stack([magn_x, magn_y, magn_z])


def electric_base(e_field, h_field, polarization, cells):
    eps_cell, sigma_cell, strength_cell, decay_cell = cells
    magn_x, magn_y, magn_z = (h_field[0], h_field[1], h_field[2])
    minus_x, minus_y = magnetic_rims(h_field)
    curl_x = magn_z - minus_y[1] - (magn_y - prev_vertical(magn_y))
    curl_y = magn_x - prev_vertical(magn_x) - (magn_z - minus_x[1])
    curl_z = magn_y - minus_x[0] - (magn_x - minus_y[0])
    curl_all = jnp.stack([curl_x, curl_y, curl_z])
    polar_new = (
        decay_cell[:, None] * polarization
        + (1.0 - decay_cell[:, None]) * strength_cell[:, None] * e_field[None]
    )
    change = jnp.sum(polar_new - polarization, axis=0)
    drive = TIME_STEP * curl_all - TIME_STEP * sigma_cell[None] * e_field - change
    return (drive, polar_new)


def electric_finish(e_field, drive, wire_term, cells):
    drive = drive.at[2].add(-TIME_STEP * wire_term)
    return e_field + drive / cells[0][None]


def on_device(
    e_field,
    h_field,
    polarization,
    material,
    eps_inf,
    conductivity,
    pole_strength,
    pole_decay,
    seg_owner,
    seg_cell,
    current,
    voltage,
    wire_gain,
    wire_cap,
):
    n_gy = lax.axis_size("gy")
    seg_count = seg_owner.shape[1]
    capacity = max(2 * seg_count // n_gy, 16)
    owner_col = seg_owner[0, :, 0]
    cell_ids = seg_cell[0]
    order = jnp.arange(seg_count, dtype=jnp.int32)
    earlier_same = (owner_col[None, :] == owner_col[:, None]) & (order[None, :] < order[:, None])
    rank_in = jnp.sum(earlier_same.astype(jnp.int32), axis=1)
    slot_at = owner_col * capacity + rank_in
    grid_shape = material.shape
    cell_total = grid_shape[0] * grid_shape[1] * grid_shape[2]
    single_zero = jnp.zeros((1,), jnp.float32)

    slot_total = n_gy * capacity
    highest = lax.Precision.HIGHEST
    slot_hot = (jnp.arange(slot_total, dtype=jnp.int32)[:, None] == slot_at[None, :]).astype(jnp.float32)
    slot_used = jnp.sum(slot_hot, axis=1)

    def to_slots(rows, fill):
        placed = jnp.einsum("fs,ts->ft", rows, slot_hot, precision=highest)
        buffer = placed + jnp.asarray(fill, jnp.float32)[:, None] * (1.0 - slot_used)[None, :]
        return buffer.reshape(rows.shape[0], n_gy, capacity).transpose(1, 0, 2)

    def exchange(blocks):
        return lax.all_to_all(blocks, "gy", split_axis=0, concat_axis=0, tiled=True)

    def from_slots(blocks):
        flat = blocks.transpose(1, 0, 2).reshape(blocks.shape[1], slot_total)
        return jnp.einsum("ft,ts->fs", flat, slot_hot, precision=highest)

    gain_row = wire_gain[0]
    cap_row = wire_cap[0]
    volt_0 = voltage[0]
    curr_0 = current[0]
    drop_0 = jnp.concatenate([volt_0[1:], single_zero]) - volt_0
    outgoing = to_slots(jnp.stack([cell_ids.astype(jnp.float32), curr_0, gain_row, drop_0]), [-1.0, 0.0, 0.0, 0.0])
    h_field = magnetic_update(e_field, h_field)
    outgoing, h_field = lax.optimization_barrier((outgoing, h_field))
    incoming = exchange(outgoing)

    material_hot = (
        material[None] == jnp.arange(eps_inf.shape[0], dtype=jnp.int32)[:, None, None, None]
    ).astype(jnp.float32)
    eps_cell = jnp.einsum("m,mxyz->xyz", eps_inf, material_hot, precision=highest)
    sigma_cell = jnp.einsum("m,mxyz->xyz", conductivity, material_hot, precision=highest)
    strength_cell = jnp.einsum("pm,mxyz->pxyz", pole_strength, material_hot, precision=highest)
    decay_cell = jnp.einsum("pm,mxyz->pxyz", pole_decay, material_hot, precision=highest)
    cells = (eps_cell, sigma_cell, strength_cell, decay_cell)

    drive, polar_next = electric_base(e_field, h_field, polarization, cells)

    recv_cells = incoming[:, 0, :].astype(jnp.int32)
    is_valid = recv_cells >= 0
    safe_cells = jnp.where(is_valid, recv_cells, 0)
    recv_curr = incoming[:, 1, :]
    recv_gain = incoming[:, 2, :]
    recv_drop = incoming[:, 3, :]
    lanes = 128
    plane_rows = cell_total // lanes
    row_hot = ((safe_cells // lanes)[:, :, None] == jnp.arange(plane_rows, dtype=jnp.int32)).astype(jnp.float32)
    row_hot = row_hot * is_valid.astype(jnp.float32)[:, :, None]
    lane_hot = (safe_cells % lanes)[:, :, None] == jnp.arange(lanes, dtype=jnp.int32)

    def sample(e_now):
        picked = jnp.einsum("scr,rl->scl", row_hot, e_now[2].reshape(plane_rows, lanes), precision=highest)
        return jnp.sum(jnp.where(lane_hot, picked, 0.0), axis=2)

    def wire_of(values):
        spread = jnp.where(lane_hot, values[:, :, None], 0.0)
        return jnp.einsum("scr,scl->rl", row_hot, spread, precision=highest).reshape(grid_shape)

    sample_0 = sample(e_field)
    curr_cell_1 = recv_curr + recv_gain * (sample_0 - recv_drop)
    e_field = electric_finish(e_field, drive, wire_of(curr_cell_1), cells)
    polarization = polar_next
    sample_1 = sample(e_field)

    back = jnp.stack([sample_0, sample_1], axis=1)
    back, e_field, h_field, polarization = lax.optimization_barrier((back, e_field, h_field, polarization))
    returned = from_slots(exchange(back))
    seg_sample_0, seg_sample_1 = returned[0], returned[1]
    curr_1 = curr_0 + gain_row * (seg_sample_0 - drop_0)
    curr_prev = jnp.concatenate([single_zero, curr_1[:-1]])
    volt_1 = volt_0 - cap_row * (curr_1 - curr_prev)
    drop_1 = jnp.concatenate([volt_1[1:], single_zero]) - volt_1
    curr_2 = curr_1 + gain_row * (seg_sample_1 - drop_1)
    curr_prev = jnp.concatenate([single_zero, curr_2[:-1]])
    volt_2 = volt_1 - cap_row * (curr_2 - curr_prev)
    h_field = magnetic_update(e_field, h_field)
    recv_curr_2 = exchange(to_slots(curr_2[None], [0.0]))

    drive, polarization = electric_base(e_field, h_field, polarization, cells)
    recv_curr_2, drive = lax.optimization_barrier((recv_curr_2, drive))
    e_field = electric_finish(e_field, drive, wire_of(recv_curr_2[:, 0, :]), cells)
    return (e_field, h_field, polarization, curr_2[None], volt_2[None])


def solution(mesh):
    return jax.shard_map(
        on_device,
        mesh=mesh,
        in_specs=(
            P(None, "gx", "gy", None),
            P(None, "gx", "gy", None),
            P(None, None, "gx", "gy", None),
            P("gx", "gy", None),
            P(),
            P(),
            P(),
            P(),
            P("gx", "gy", None),
            P("gx", "gy"),
            P("gx", "gy"),
            P("gx", "gy"),
            P("gx", "gy"),
            P("gx", "gy"),
        ),
        out_specs=(
            P(None, "gx", "gy", None),
            P(None, "gx", "gy", None),
            P(None, None, "gx", "gy", None),
            P("gx", "gy"),
            P("gx", "gy"),
        ),
        check_vma=False,
    )
```
